256 devices in a mesh: req: 4 (over x), tp: 64 (over z, y, core).
Axes of the slice: x: 4, y: 4, z: 8, core: 2. Of those that a mesh axis runs over, the one named last changes fastest.
Arguments:
- hidden: bfloat16 [256, 4096], P('req', 'tp'), may hold values from -6 to 6
- norm_gain: bfloat16 [4096], P('tp'), may hold values from 0.099609375 to 1.8984375
- w_qkv: bfloat16 [4096, 5120], P('tp'), may hold values from -0.1875 to 0.1875
- w_out: bfloat16 [4096, 4096], P('tp'), may hold values from -0.09375 to 0.09375
- cache_keys: bfloat16 [4, 65536, 512], P('req', 'tp')
- cache_values: bfloat16 [4, 65536, 512], P('req', 'tp'), may hold values from -6 to 6
- parents: int32 [4, 64], P('req'), may hold values from -1 to 62, as said below
- draft_counts: int32 [4], P('req'), may hold values from 1 to 64, as said below
- cache_lengths: int32 [4], P('req'), may hold values from 1 to 65536, as said below
Outputs:
- updated: bfloat16 [256, 4096], P('req', 'tp')
The draws below stay inside these ranges and needn't reach their ends.
Inputs may be any that keep to these rules, and one draw needn't show every extreme that they name: parents[r, 0] = -1 and 0 <= parents[r, i] < i for i >= 1. `draft_counts`: some request has all 64 tree tokens live. `cache_lengths`: some request has a full cache of 65536 positions.
All inputs are finite; a program needn't handle non-finite values.
Results may differ from the reference program's by a relative error of at most 0.0065.
The reference program's roundings to bfloat16 on the way count: a program that leaves them out, or rounds other values in their place, can miss the bound.
Values may be sent and summed in bfloat16 or wider, within the bound.
No kernel may reach another device: no remote copies, remote signals or barrier semaphores. Data moves between devices by JAX's collectives and lax.ppermute only.
A program may use at most 64 MiB of HBM per device.

```python
import jax
import jax.numpy as jnp
from jax import lax

D = 4096
HEADS = 32
KV_HEADS = 4
HEAD = 128
TREE = 64
REQUESTS = 4
CACHE = 65536
TOKENS = 256


def draw_cache_keys(key, part):
    base_key = jax.random.fold_in(key, 0)
    shape = (REQUESTS, CACHE, KV_HEADS * HEAD)
    values = 1.5 * jax.random.normal(base_key, shape, jnp.float32)
    return values.astype(jnp.bfloat16)


def draw_parents(key, part):
    places = jnp.arange(TREE, dtype=jnp.int32)
    upper = jnp.maximum(places, 1)
    chosen = jax.random.randint(key, (REQUESTS, TREE), 0, upper[None, :])
    return jnp.where(places[None, :] == 0, -1, chosen).astype(jnp.int32)


def draw_draft_counts(key, part):
    count_key, full_key = jax.random.split(jax.random.fold_in(key, 11))
    counts = jax.random.randint(count_key, (REQUESTS,), 1, TREE + 1)
    fullest = jax.random.randint(full_key, (), 0, REQUESTS)
    return jnp.where(jnp.arange(REQUESTS) == fullest, TREE, counts).astype(jnp.int32)


def draw_cache_lengths(key, part):
    length_key, full_key = jax.random.split(jax.random.fold_in(key, 23))
    lengths = jax.random.randint(length_key, (REQUESTS,), 1, CACHE + 1)
    longest = jax.random.randint(full_key, (), 0, REQUESTS)
    return jnp.where(jnp.arange(REQUESTS) == longest, CACHE, lengths).astype(jnp.int32)


def steps_of(key, dims, cuts, low, high):
    factor_of = 1.0
    for dim, blocks in cuts:
        steps = jax.random.uniform(jax.random.fold_in(jax.random.fold_in(key, 6), dim), (blocks,), jnp.float32, low / len(cuts), high / len(cuts))
        factor_of = factor_of * jnp.repeat(jnp.exp(steps), dims[dim] // blocks).reshape((-1,) + (1,) * (len(dims) - 1 - dim))
    return factor_of


def centred(rng, extent, spread, reach, cuts=(), held_as=jnp.bfloat16):
    factor_of = steps_of(rng, extent, cuts, -0.22, 0.18) if cuts else 1.0
    values = jax.random.normal(rng, extent, jnp.float32) * spread * factor_of
    return jnp.minimum(jnp.maximum(values, -reach), reach).astype(held_as)


def setup_inputs(seed: int = 0) -> dict:
    splits = jax.random.split(jax.random.key(seed), 10)
    return {
        "hidden": centred(splits[0], (TOKENS, D), 1.0, 6.0, ((0, 4), (1, 64))),
        "norm_gain": jnp.clip(1.0 + 0.18 * jax.random.normal(splits[1], (D,), jnp.float32), 0.099609375, 1.8984375).astype(jnp.bfloat16),
        "w_qkv": centred(splits[2], (D, D + 2 * KV_HEADS * HEAD), (D // 4) ** -0.5, 0.1875, ((0, 64),)),
        "w_out": centred(splits[3], (D, D), D ** -0.5, 0.09375, ((0, 64),)),
        "cache_keys": draw_cache_keys(jax.random.fold_in(splits[9], 71), 0),
        "cache_values": centred(splits[5], (REQUESTS, CACHE, KV_HEADS * HEAD), 1.0, 6.0, ((0, 4), (1, 64))),
        "parents": draw_parents(jax.random.fold_in(splits[9], 71), 0),
        "draft_counts": draw_draft_counts(jax.random.fold_in(splits[9], 71), 0),
        "cache_lengths": draw_cache_lengths(jax.random.fold_in(splits[9], 71), 0),
    }


NEGATIVE = -1e+30

def tree_reach(parents):
    width = parents.shape[1]
    places = jnp.arange(width, dtype=jnp.int32)
    parent_link = (parents[:, :, None] == places[None, None, :]).astype(jnp.float32)
    identity = (places[:, None] == places[None, :]).astype(jnp.float32)
    reached = jnp.minimum(parent_link + identity[None], 1.0)
    for rounds in range(width.bit_length()):
        reached = jnp.minimum(jnp.einsum('rij,rjk->rik', reached, reached, precision=lax.Precision.HIGHEST), 1.0)
    return reached

def reference(hidden, norm_gain, w_qkv, w_out, cache_keys, cache_values, parents, draft_counts, cache_lengths):
    inputs = hidden.astype(jnp.float32)
    scaled = (inputs * norm_gain.astype(jnp.float32)[None, :]).astype(jnp.bfloat16)
    raw = jnp.dot(scaled, w_qkv, preferred_element_type=jnp.float32)
    square_sum = lax.optimization_barrier(jnp.sum(inputs * inputs, axis=1))
    qkv = (raw * lax.rsqrt(square_sum / D + 1e-05)[:, None]).astype(jnp.bfloat16)
    kv_width = KV_HEADS * HEAD
    groups = HEADS // KV_HEADS
    queries = qkv[:, :D].reshape(REQUESTS, TREE, KV_HEADS, groups, HEAD)
    new_keys = qkv[:, D:D + kv_width].reshape(REQUESTS, TREE, KV_HEADS, HEAD)
    new_values = qkv[:, D + kv_width:].reshape(REQUESTS, TREE, KV_HEADS, HEAD)
    reached = tree_reach(parents)
    places = jnp.arange(TREE, dtype=jnp.int32)
    tree_mask = (reached > 0.5) & (places[None, None, :] < draft_counts[:, None, None])
    scale = HEAD ** (-0.5)
    positions = jnp.arange(CACHE, dtype=jnp.int32)

    def one_request(items):
        query_block, keys, values, fresh_keys, fresh_values, length, mask = items
        valid = positions < length

        def one_head(head_items):
            query_head, key_head, value_head, fresh_key, fresh_value = head_items
            query_float = query_head.astype(jnp.float32)
            cache_scores = jnp.einsum('tgd,pd->tgp', query_float, key_head.astype(jnp.float32)) * scale
            cache_scores = jnp.where(valid[None, None, :], cache_scores, NEGATIVE)
            tree_scores = jnp.einsum('tgd,ud->tgu', query_float, fresh_key.astype(jnp.float32)) * scale
            tree_scores = jnp.where(mask[:, None, :], tree_scores, NEGATIVE)
            top = jnp.maximum(lax.optimization_barrier(jnp.max(cache_scores, axis=-1)), lax.optimization_barrier(jnp.max(tree_scores, axis=-1)))
            cache_exp = jnp.exp(cache_scores - top[..., None])
            tree_exp = jnp.exp(tree_scores - top[..., None])
            totals = lax.optimization_barrier(jnp.sum(cache_exp, axis=-1)) + lax.optimization_barrier(jnp.sum(tree_exp, axis=-1))
            mixed = jnp.einsum('tgp,pd->tgd', cache_exp.astype(jnp.bfloat16).astype(jnp.float32), value_head.astype(jnp.float32))
            mixed = mixed + jnp.einsum('tgu,ud->tgd', tree_exp.astype(jnp.bfloat16).astype(jnp.float32), fresh_value.astype(jnp.float32))
            return mixed / totals[..., None]
        head_inputs = (jnp.swapaxes(query_block, 0, 1), jnp.swapaxes(keys.reshape(CACHE, KV_HEADS, HEAD), 0, 1), jnp.swapaxes(values.reshape(CACHE, KV_HEADS, HEAD), 0, 1), jnp.swapaxes(fresh_keys, 0, 1), jnp.swapaxes(fresh_values, 0, 1))
        head_out = lax.map(one_head, head_inputs)
        return jnp.swapaxes(head_out, 0, 1).reshape(TREE, D)
    attended = lax.map(one_request, (queries, cache_keys, cache_values, new_keys, new_values, cache_lengths, tree_mask))
    attended = attended.reshape(TOKENS, D).astype(jnp.bfloat16)
    return (inputs + jnp.dot(attended, w_out, preferred_element_type=jnp.float32)).astype(jnp.bfloat16)
```

```python
import jax
import jax.numpy as jnp
from jax import lax
from jax.sharding import PartitionSpec as P

HEADS = 32
KV_HEADS = 4
HEAD = 128


NEGATIVE = -1e30


def tree_reach(parents):
    width = parents.shape[1]
    places = jnp.arange(width, dtype=jnp.int32)
    parent_link = (parents[:, :, None] == places[None, None, :]).astype(jnp.float32)
    identity = (places[:, None] == places[None, :]).astype(jnp.float32)
    reached = jnp.minimum(parent_link + identity[None], 1.0)
    for rounds in range(width.bit_length()):
        reached = jnp.minimum(
            jnp.einsum("rij,rjk->rik", reached, reached, precision=lax.Precision.HIGHEST), 1.0
        )
    return reached


def spread(pieces):
    return lax.all_to_all(pieces, "tp", 0, 0, tiled=True)


def on_device(
    hidden, norm_gain, w_qkv, w_out, cache_keys, cache_values, parents, draft_counts, cache_lengths
):
    tp_count = lax.axis_size("tp")
    tp_rank = lax.axis_index("tp")
    model_width = w_out.shape[1]
    kv_width = KV_HEADS * HEAD
    groups = HEADS // KV_HEADS
    tree = parents.shape[1]
    places_dev = cache_keys.shape[1]
    inputs = hidden.astype(jnp.float32)
    all_rows = inputs.shape[0]
    own_count = all_rows // tp_count
    proj_width = w_qkv.shape[1]

    scaled = (inputs * norm_gain.astype(jnp.float32)[None, :]).astype(jnp.bfloat16)
    local_squares = jnp.sum(inputs * inputs, axis=1)
    partial = jnp.dot(scaled, w_qkv, preferred_element_type=jnp.float32)
    extended = jnp.concatenate(
        [partial, jnp.broadcast_to(local_squares[:, None], (all_rows, 128))], axis=1
    )
    gathered = spread(extended.reshape(tp_count, own_count, proj_width + 128))
    own_sum = jnp.sum(gathered, axis=0)
    square_sum = own_sum[:, proj_width]
    own_qkv = (
        own_sum[:, :proj_width] * lax.rsqrt(square_sum / model_width + 1e-05)[:, None]
    ).astype(jnp.bfloat16)
    own_queries = own_qkv[:, :model_width]
    query = spread(
        jnp.broadcast_to(own_queries[None], (tp_count, own_count, model_width))
    ).reshape(all_rows, model_width)
    own_tokens = own_qkv[:, model_width:]
    own_keys = own_tokens[:, :kv_width].reshape(own_count, KV_HEADS, HEAD)
    own_values = own_tokens[:, kv_width:].reshape(own_count, KV_HEADS, HEAD)

    scale = HEAD ** (-0.5)
    key_index = tp_rank * own_count + jnp.arange(own_count, dtype=jnp.int32)
    key_place = key_index % tree
    reached = tree_reach(parents).reshape(all_rows, tree)
    column_pick = (jnp.arange(tree, dtype=jnp.int32)[:, None] == key_place[None, :]).astype(
        jnp.float32
    )
    on_path = jnp.dot(reached, column_pick, precision=lax.Precision.HIGHEST) > 0.5
    tree_mask = on_path & (key_place < draft_counts[0])[None, :]

    query_heads = query.reshape(all_rows, KV_HEADS, groups, HEAD)
    positions = tp_rank * places_dev + jnp.arange(places_dev, dtype=jnp.int32)
    valid = positions < cache_lengths[0]
    cache_scores = (
        jnp.einsum(
            "tkgd,pkd->tkgp",
            query_heads,
            cache_keys[0].reshape(places_dev, KV_HEADS, HEAD),
            preferred_element_type=jnp.float32,
        )
        * scale
    )
    cache_scores = jnp.where(valid[None, None, None, :], cache_scores, NEGATIVE)
    tree_scores = (
        jnp.einsum("tkgd,ukd->tkgu", query_heads, own_keys, preferred_element_type=jnp.float32)
        * scale
    )
    tree_scores = jnp.where(tree_mask[:, None, None, :], tree_scores, NEGATIVE)
    local_top = jnp.maximum(jnp.max(cache_scores, axis=-1), jnp.max(tree_scores, axis=-1))
    cache_exp = jnp.where(
        valid[None, None, None, :], jnp.exp(cache_scores - local_top[..., None]), 0.0
    )
    tree_exp = jnp.where(
        tree_mask[:, None, None, :], jnp.exp(tree_scores - local_top[..., None]), 0.0
    )
    totals = jnp.sum(cache_exp, axis=-1) + jnp.sum(tree_exp, axis=-1)
    mixed = jnp.einsum(
        "tkgp,pkd->tkgd",
        cache_exp.astype(jnp.bfloat16),
        cache_values[0].reshape(places_dev, KV_HEADS, HEAD),
        preferred_element_type=jnp.float32,
    ) + jnp.einsum(
        "tkgu,ukd->tkgd",
        tree_exp.astype(jnp.bfloat16),
        own_values,
        preferred_element_type=jnp.float32,
    )

    columns = w_out.shape[0]
    per_head = HEAD // columns
    owner_mixed = jnp.swapaxes(mixed.reshape(all_rows, tp_count, columns), 0, 1)
    owner_top = jnp.repeat(jnp.swapaxes(local_top.reshape(all_rows, HEADS), 0, 1), per_head, 0)
    owner_totals = jnp.repeat(jnp.swapaxes(totals.reshape(all_rows, HEADS), 0, 1), per_head, 0)
    packed = jnp.concatenate(
        [owner_mixed, owner_top[..., None], owner_totals[..., None]], axis=2
    )
    got = spread(packed)
    source_top = got[:, :, columns]
    top = jnp.max(source_top, axis=0)
    rescale = jnp.exp(source_top - top[None])
    total = jnp.sum(rescale * got[:, :, columns + 1], axis=0)
    mixed_cols = jnp.sum(rescale[..., None] * got[:, :, :columns], axis=0)
    attended = (mixed_cols / total[:, None]).astype(jnp.bfloat16)

    partial_terms = jnp.dot(attended, w_out, preferred_element_type=jnp.float32)
    out_cols = model_width // tp_count
    terms = spread(jnp.swapaxes(partial_terms.reshape(all_rows, tp_count, out_cols), 0, 1))
    projected = jnp.sum(terms, axis=0)
    return (inputs + projected).astype(jnp.bfloat16)


def solution(mesh):
    placed = (
        P("req", "tp"),
        P("tp"),
        P("tp", None),
        P("tp", None),
        P("req", "tp", None),
        P("req", "tp", None),
        P("req", None),
        P("req"),
        P("req"),
    )
    return jax.shard_map(
        on_device, mesh=mesh, in_specs=placed, out_specs=P("req", "tp"), check_vma=False
    )
```

```python
import jax
import jax.numpy as jnp
from jax import lax
from jax.sharding import PartitionSpec as P

HEADS = 32
KV_HEADS = 4
HEAD = 128


NEGATIVE = -1e30


def tree_reach(parents):
    width = parents.shape[1]
    places = jnp.arange(width, dtype=jnp.int32)
    parent_link = (parents[:, :, None] == places[None, None, :]).astype(jnp.float32)
    identity = (places[:, None] == places[None, :]).astype(jnp.float32)
    reached = jnp.minimum(parent_link + identity[None], 1.0)
    for rounds in range(width.bit_length()):
        reached = jnp.minimum(
            jnp.einsum("rij,rjk->rik", reached, reached, precision=lax.Precision.HIGHEST), 1.0
        )
    return reached


def spread(pieces):
    return lax.all_to_all(pieces, "tp", 0, 0, tiled=True)


def on_device(
    hidden, norm_gain, w_qkv, w_out, cache_keys, cache_values, parents, draft_counts, cache_lengths
):
    tp_count = lax.axis_size("tp")
    tp_rank = lax.axis_index("tp")
    model_width = w_out.shape[1]
    kv_width = KV_HEADS * HEAD
    groups = HEADS // KV_HEADS
    tree = parents.shape[1]
    places_dev = cache_keys.shape[1]
    inputs = hidden.astype(jnp.float32)
    all_rows = inputs.shape[0]
    own_count = all_rows // tp_count
    proj_width = w_qkv.shape[1]

    scaled = (inputs * norm_gain.astype(jnp.float32)[None, :]).astype(jnp.bfloat16)
    local_squares = jnp.sum(inputs * inputs, axis=1)
    partial = jnp.dot(scaled, w_qkv, preferred_element_type=jnp.float32)
    extended = jnp.concatenate(
        [partial, jnp.broadcast_to(local_squares[:, None], (all_rows, 128))], axis=1
    )
    gathered = spread(extended.reshape(tp_count, own_count, proj_width + 128))
    own_sum = jnp.sum(gathered, axis=0)
    square_sum = own_sum[:, proj_width]
    own_qkv = (
        own_sum[:, :proj_width] * lax.rsqrt(square_sum / model_width + 1e-05)[:, None]
    ).astype(jnp.bfloat16)
    own_queries = own_qkv[:, :model_width]
    query = spread(
        jnp.broadcast_to(own_queries[None], (tp_count, own_count, model_width))
    ).reshape(all_rows, model_width)
    own_tokens = own_qkv[:, model_width:]
    own_keys = own_tokens[:, :kv_width].reshape(own_count, KV_HEADS, HEAD)
    own_values = own_tokens[:, kv_width:].reshape(own_count, KV_HEADS, HEAD)

    scale = HEAD ** (-0.5)
    key_index = tp_rank * own_count + jnp.arange(own_count, dtype=jnp.int32)
    key_place = key_index % tree
    reached = tree_reach(parents).reshape(all_rows, tree)
    column_pick = (jnp.arange(tree, dtype=jnp.int32)[:, None] == key_place[None, :]).astype(
        jnp.float32
    )
    on_path = jnp.dot(reached, column_pick, precision=lax.Precision.HIGHEST) > 0.5
    tree_mask = on_path & (key_place < draft_counts[0])[None, :]

    query_heads = query.reshape(all_rows, KV_HEADS, groups, HEAD)
    positions = tp_rank * places_dev + jnp.arange(places_dev, dtype=jnp.int32)
    valid = positions < cache_lengths[0]
    cache_scores = (
        jnp.einsum(
            "tkgd,pkd->tkgp",
            query_heads,
            cache_keys[0].reshape(places_dev, KV_HEADS, HEAD),
            preferred_element_type=jnp.float32,
        )
        * scale
    )
    cache_scores = jnp.where(valid[None, None, None, :], cache_scores, NEGATIVE)
    tree_scores = (
        jnp.einsum("tkgd,ukd->tkgu", query_heads, own_keys, preferred_element_type=jnp.float32)
        * scale
    )
    tree_scores = jnp.where(tree_mask[:, None, None, :], tree_scores, NEGATIVE)
    local_top = jnp.maximum(jnp.max(cache_scores, axis=-1), jnp.max(tree_scores, axis=-1))
    cache_exp = jnp.where(
        valid[None, None, None, :], jnp.exp(cache_scores - local_top[..., None]), 0.0
    )
    tree_exp = jnp.where(
        tree_mask[:, None, None, :], jnp.exp(tree_scores - local_top[..., None]), 0.0
    )
    totals = jnp.sum(cache_exp, axis=-1) + jnp.sum(tree_exp, axis=-1)
    mixed = jnp.einsum(
        "tkgp,pkd->tkgd",
        cache_exp.astype(jnp.bfloat16),
        cache_values[0].reshape(places_dev, KV_HEADS, HEAD),
        preferred_element_type=jnp.float32,
    ) + jnp.einsum(
        "tkgu,ukd->tkgd",
        tree_exp.astype(jnp.bfloat16),
        own_values,
        preferred_element_type=jnp.float32,
    )

    columns = w_out.shape[0]
    per_head = HEAD // columns
    owner_mixed = jnp.swapaxes(mixed.reshape(all_rows, tp_count, columns), 0, 1)
    owner_top = jnp.repeat(jnp.swapaxes(local_top.reshape(all_rows, HEADS), 0, 1), per_head, 0)
    owner_totals = jnp.repeat(jnp.swapaxes(totals.reshape(all_rows, HEADS), 0, 1), per_head, 0)
    packed = jnp.concatenate(
        [owner_mixed.reshape(tp_count, all_rows * columns), owner_top, owner_totals], axis=1
    )
    got = spread(packed)
    flat = all_rows * columns
    source_top = got[:, flat : flat + all_rows]
    top = jnp.max(source_top, axis=0)
    rescale = jnp.exp(source_top - top[None])
    total = jnp.sum(rescale * got[:, flat + all_rows :], axis=0)
    source_mixed = got[:, :flat].reshape(tp_count, all_rows, columns)
    mixed_cols = jnp.sum(rescale[..., None] * source_mixed, axis=0)
    attended = (mixed_cols / total[:, None]).astype(jnp.bfloat16)

    partial_terms = jnp.dot(attended, w_out, preferred_element_type=jnp.float32)
    out_cols = model_width // tp_count
    owner_terms = jnp.swapaxes(partial_terms.reshape(all_rows, tp_count, out_cols), 0, 1)
    terms = spread(owner_terms.reshape(tp_count, all_rows * out_cols))
    projected = jnp.sum(terms, axis=0).reshape(all_rows, out_cols)
    return (inputs + projected).astype(jnp.bfloat16)


def solution(mesh):
    placed = (
        P("req", "tp"),
        P("tp"),
        P("tp", None),
        P("tp", None),
        P("req", "tp", None),
        P("req", "tp", None),
        P("req", None),
        P("req"),
        P("req"),
    )
    return jax.shard_map(
        on_device, mesh=mesh, in_specs=placed, out_specs=P("req", "tp"), check_vma=False
    )
```

```python
import jax
import jax.numpy as jnp
from jax import lax
from jax.experimental import pallas as pl
from jax.experimental.pallas import tpu as pltpu
from jax.sharding import PartitionSpec as P

HEADS = 32
KV_HEADS = 4
HEAD = 128


NEGATIVE = -1e30


def tree_reach(parents):
    width = parents.shape[1]
    places = jnp.arange(width, dtype=jnp.int32)
    parent_link = (parents[:, :, None] == places[None, None, :]).astype(jnp.float32)
    identity = (places[:, None] == places[None, :]).astype(jnp.float32)
    reached = jnp.minimum(parent_link + identity[None], 1.0)
    for rounds in range(width.bit_length()):
        reached = jnp.minimum(
            jnp.einsum("rij,rjk->rik", reached, reached, precision=lax.Precision.HIGHEST), 1.0
        )
    return reached


def attention_kernel(limit_ref, q_ref, k_ref, v_ref, ts_ref, tv_ref, o_ref, m_ref, l_ref):
    rows, places = q_ref.shape[1], k_ref.shape[0]
    scale = HEAD ** (-0.5)
    scores = (
        lax.dot_general(
            q_ref[0], k_ref[...], (((1,), (1,)), ((), ())), preferred_element_type=jnp.float32
        )
        * scale
    )
    valid = lax.broadcasted_iota(jnp.int32, (rows, places), 1) < limit_ref[0]
    scores = jnp.where(valid, scores, NEGATIVE)
    tree_score = ts_ref[0]
    top = jnp.maximum(jnp.max(scores, axis=1, keepdims=True), tree_score)
    shift = jnp.where(top > 0.5 * NEGATIVE, top, 0.0)
    weights = jnp.exp(scores - shift)
    tree_weight = jnp.exp(tree_score - shift)
    m_ref[0] = top
    l_ref[0] = jnp.sum(weights, axis=1, keepdims=True) + tree_weight
    o_ref[0] = jnp.dot(
        weights.astype(jnp.bfloat16), v_ref[...], preferred_element_type=jnp.float32
    ) + tree_weight.astype(jnp.bfloat16).astype(jnp.float32) * tv_ref[0].astype(jnp.float32)


def local_attention(limit, query, keys, values, tree_scores, own_values):
    rows = query.shape[1]
    places = keys.shape[0]
    return pl.pallas_call(
        attention_kernel,
        grid_spec=pltpu.PrefetchScalarGridSpec(
            num_scalar_prefetch=1,
            grid=(KV_HEADS,),
            in_specs=[
                pl.BlockSpec((1, rows, HEAD), lambda k, lim: (k, 0, 0)),
                pl.BlockSpec((places, HEAD), lambda k, lim: (0, k)),
                pl.BlockSpec((places, HEAD), lambda k, lim: (0, k)),
                pl.BlockSpec((1, rows, 1), lambda k, lim: (k, 0, 0)),
                pl.BlockSpec((1, 1, HEAD), lambda k, lim: (k, 0, 0)),
            ],
            out_specs=[
                pl.BlockSpec((1, rows, HEAD), lambda k, lim: (k, 0, 0)),
                pl.BlockSpec((1, rows, 1), lambda k, lim: (k, 0, 0)),
                pl.BlockSpec((1, rows, 1), lambda k, lim: (k, 0, 0)),
            ],
        ),
        out_shape=[
            jax.ShapeDtypeStruct((KV_HEADS, rows, HEAD), jnp.float32),
            jax.ShapeDtypeStruct((KV_HEADS, rows, 1), jnp.float32),
            jax.ShapeDtypeStruct((KV_HEADS, rows, 1), jnp.float32),
        ],
    )(limit, query, keys, values, tree_scores, own_values)


def split3(values):
    high = lax.reduce_precision(values, exponent_bits=8, mantissa_bits=7)
    rest = values - high
    middle = lax.reduce_precision(rest, exponent_bits=8, mantissa_bits=7)
    low = rest - middle
    return [high.astype(jnp.bfloat16), middle.astype(jnp.bfloat16), low.astype(jnp.bfloat16)]


def join3(high, middle, low):
    return high.astype(jnp.float32) + middle.astype(jnp.float32) + low.astype(jnp.float32)


def spread(pieces):
    return lax.all_to_all(pieces, "tp", 0, 0, tiled=True)


def on_device(
    hidden, norm_gain, w_qkv, w_out, cache_keys, cache_values, parents, draft_counts, cache_lengths
):
    tp_count = lax.axis_size("tp")
    tp_rank = lax.axis_index("tp")
    model_width = w_out.shape[1]
    kv_width = KV_HEADS * HEAD
    groups = HEADS // KV_HEADS
    tree = parents.shape[1]
    places_dev = cache_keys.shape[1]
    inputs = hidden.astype(jnp.float32)
    all_rows = inputs.shape[0]
    own_count = all_rows // tp_count
    proj_width = w_qkv.shape[1]

    scaled = (inputs * norm_gain.astype(jnp.float32)[None, :]).astype(jnp.bfloat16)
    local_squares = jnp.sum(inputs * inputs, axis=1)
    partial = jnp.dot(scaled, w_qkv, preferred_element_type=jnp.float32)
    extended = jnp.concatenate(
        [partial, jnp.broadcast_to(local_squares[:, None], (all_rows, 128))], axis=1
    )
    gathered = spread(extended.reshape(tp_count, own_count, proj_width + 128))
    own_sum = jnp.sum(gathered, axis=0)
    square_sum = own_sum[:, proj_width]
    own_qkv = (
        own_sum[:, :proj_width] * lax.rsqrt(square_sum / model_width + 1e-05)[:, None]
    ).astype(jnp.bfloat16)
    own_queries = own_qkv[:, :model_width]
    lanes = own_count * model_width // 128
    query = spread(
        jnp.broadcast_to(own_queries.reshape(1, lanes, 128), (tp_count, lanes, 128))
    ).reshape(all_rows, model_width)
    own_tokens = own_qkv[:, model_width:]
    own_keys = own_tokens[:, :kv_width].reshape(own_count, KV_HEADS, HEAD)
    own_values = own_tokens[:, kv_width:].reshape(own_count, KV_HEADS, HEAD)

    scale = HEAD ** (-0.5)
    key_index = tp_rank * own_count + jnp.arange(own_count, dtype=jnp.int32)
    key_place = key_index % tree
    reached = tree_reach(parents).reshape(all_rows, tree)
    column_pick = (jnp.arange(tree, dtype=jnp.int32)[:, None] == key_place[None, :]).astype(
        jnp.float32
    )
    on_path = jnp.dot(reached, column_pick, precision=lax.Precision.HIGHEST) > 0.5
    tree_mask = on_path & (key_place < draft_counts[0])[None, :]

    query_heads = query.reshape(all_rows, KV_HEADS, groups, HEAD)
    tree_scores = (
        jnp.einsum("tkgd,ukd->tkgu", query_heads, own_keys, preferred_element_type=jnp.float32)
        * scale
    )
    tree_scores = jnp.where(tree_mask[:, None, None, :], tree_scores, NEGATIVE)
    limit = (cache_lengths[:1] - tp_rank * places_dev).astype(jnp.int32)
    head_rows = jnp.transpose(query_heads, (1, 2, 0, 3)).reshape(KV_HEADS, groups * all_rows, HEAD)
    head_mixed, top_parts, total_parts = local_attention(
        limit,
        head_rows,
        cache_keys[0],
        cache_values[0],
        jnp.transpose(tree_scores[..., 0], (1, 2, 0)).reshape(KV_HEADS, groups * all_rows, 1),
        own_values[0].reshape(KV_HEADS, 1, HEAD),
    )
    local_top = top_parts.reshape(HEADS, all_rows)
    totals = total_parts.reshape(HEADS, all_rows)

    columns = w_out.shape[0]
    per_head = HEAD // columns
    halves = HEAD // columns
    owner_mixed = jnp.swapaxes(
        head_mixed.reshape(HEADS, all_rows, halves, columns), 1, 2
    ).reshape(tp_count, all_rows * columns)
    owner_top = jnp.repeat(local_top, per_head, 0)
    owner_totals = jnp.repeat(totals, per_head, 0)
    packed = jnp.concatenate(
        [owner_mixed.astype(jnp.bfloat16)]
        + split3(owner_top)
        + split3(owner_totals)
        + [jnp.zeros((tp_count, 128 - (6 * all_rows) % 128), jnp.bfloat16)],
        axis=1,
    )
    got = spread(packed.reshape(tp_count, -1, 128)).reshape(tp_count, -1)
    flat = all_rows * columns
    piece = [got[:, flat + i * all_rows : flat + (i + 1) * all_rows] for i in range(6)]
    source_top = join3(*piece[:3])
    top = jnp.max(source_top, axis=0)
    rescale = jnp.exp(source_top - top[None])
    total = jnp.sum(rescale * join3(*piece[3:]), axis=0)
    source_mixed = got[:, :flat].reshape(tp_count, all_rows, columns).astype(jnp.float32)
    mixed_cols = jnp.sum(rescale[..., None] * source_mixed, axis=0)
    attended = (mixed_cols / total[:, None]).astype(jnp.bfloat16)

    partial_terms = jnp.dot(attended, w_out, preferred_element_type=jnp.float32)
    out_cols = model_width // tp_count
    owner_terms = jnp.swapaxes(partial_terms.reshape(all_rows, tp_count, out_cols), 0, 1)
    terms = spread(
        owner_terms.reshape(tp_count, all_rows * out_cols // 128, 128).astype(jnp.bfloat16)
    )
    projected = jnp.sum(terms.astype(jnp.float32), axis=0).reshape(all_rows, out_cols)
    return (inputs + projected).astype(jnp.bfloat16)


def solution(mesh):
    placed = (
        P("req", "tp"),
        P("tp"),
        P("tp", None),
        P("tp", None),
        P("req", "tp", None),
        P("req", "tp", None),
        P("req", None),
        P("req"),
        P("req"),
    )
    return jax.shard_map(
        on_device, mesh=mesh, in_specs=placed, out_specs=P("req", "tp"), check_vma=False
    )
```

```python
import jax
import jax.numpy as jnp
from jax import lax
from jax.experimental import pallas as pl
from jax.experimental.pallas import tpu as pltpu
from jax.sharding import PartitionSpec as P

HEADS = 32
KV_HEADS = 4
HEAD = 128


NEGATIVE = -1e30


def tree_reach(parents):
    width = parents.shape[1]
    places = jnp.arange(width, dtype=jnp.int32)
    parent_link = (parents[:, :, None] == places[None, None, :]).astype(jnp.float32)
    identity = (places[:, None] == places[None, :]).astype(jnp.float32)
    reached = jnp.minimum(parent_link + identity[None], 1.0)
    for rounds in range(width.bit_length()):
        reached = jnp.minimum(
            jnp.einsum("rij,rjk->rik", reached, reached, precision=lax.Precision.HIGHEST), 1.0
        )
    return reached


def attention_kernel(limit_ref, q_ref, k_ref, v_ref, ts_ref, o_ref, m_ref, l_ref):
    rows, places = q_ref.shape[1], k_ref.shape[0]
    scale = HEAD ** (-0.5)
    scores = (
        lax.dot_general(
            k_ref[...], q_ref[0], (((1,), (1,)), ((), ())), preferred_element_type=jnp.float32
        )
        * scale
    )
    valid = lax.broadcasted_iota(jnp.int32, (places, rows), 0) < limit_ref[0]
    scores = jnp.where(valid, scores, NEGATIVE)
    tree_score = ts_ref[0]
    top = jnp.maximum(jnp.max(scores, axis=0, keepdims=True), tree_score)
    shift = jnp.where(top > 0.5 * NEGATIVE, top, 0.0)
    weights = jnp.exp(scores - shift)
    m_ref[0] = top
    l_ref[0] = jnp.sum(weights, axis=0, keepdims=True) + jnp.exp(tree_score - shift)
    o_ref[0] = lax.dot_general(
        weights.astype(jnp.bfloat16),
        v_ref[...],
        (((0,), (0,)), ((), ())),
        preferred_element_type=jnp.float32,
    )


def local_attention(limit, query, keys, values, tree_scores):
    rows = query.shape[1]
    places = keys.shape[0]
    return pl.pallas_call(
        attention_kernel,
        grid_spec=pltpu.PrefetchScalarGridSpec(
            num_scalar_prefetch=1,
            grid=(KV_HEADS,),
            in_specs=[
                pl.BlockSpec((1, rows, HEAD), lambda k, lim: (k, 0, 0)),
                pl.BlockSpec((places, HEAD), lambda k, lim: (0, k)),
                pl.BlockSpec((places, HEAD), lambda k, lim: (0, k)),
                pl.BlockSpec((1, 1, rows), lambda k, lim: (k, 0, 0)),
            ],
            out_specs=[
                pl.BlockSpec((1, rows, HEAD), lambda k, lim: (k, 0, 0)),
                pl.BlockSpec((1, 1, rows), lambda k, lim: (k, 0, 0)),
                pl.BlockSpec((1, 1, rows), lambda k, lim: (k, 0, 0)),
            ],
        ),
        out_shape=[
            jax.ShapeDtypeStruct((KV_HEADS, rows, HEAD), jnp.float32),
            jax.ShapeDtypeStruct((KV_HEADS, 1, rows), jnp.float32),
            jax.ShapeDtypeStruct((KV_HEADS, 1, rows), jnp.float32),
        ],
    )(limit, query, keys, values, tree_scores)


def split3(values):
    high = lax.reduce_precision(values, exponent_bits=8, mantissa_bits=7)
    rest = values - high
    middle = lax.reduce_precision(rest, exponent_bits=8, mantissa_bits=7)
    low = rest - middle
    return [high.astype(jnp.bfloat16), middle.astype(jnp.bfloat16), low.astype(jnp.bfloat16)]


def join3(high, middle, low):
    return high.astype(jnp.float32) + middle.astype(jnp.float32) + low.astype(jnp.float32)


def spread(pieces):
    return lax.all_to_all(pieces, "tp", 0, 0, tiled=True)


def on_device(
    hidden, norm_gain, w_qkv, w_out, cache_keys, cache_values, parents, draft_counts, cache_lengths
):
    tp_count = lax.axis_size("tp")
    tp_rank = lax.axis_index("tp")
    model_width = w_out.shape[1]
    kv_width = KV_HEADS * HEAD
    groups = HEADS // KV_HEADS
    tree = parents.shape[1]
    places_dev = cache_keys.shape[1]
    inputs = hidden.astype(jnp.float32)
    all_rows = inputs.shape[0]
    own_count = all_rows // tp_count
    proj_width = w_qkv.shape[1]

    scaled = (inputs * norm_gain.astype(jnp.float32)[None, :]).astype(jnp.bfloat16)
    local_squares = jnp.sum(inputs * inputs, axis=1)
    partial = jnp.dot(scaled, w_qkv, preferred_element_type=jnp.float32)
    extended = jnp.concatenate(
        [partial, jnp.broadcast_to(local_squares[:, None], (all_rows, 128))], axis=1
    )
    gathered = spread(extended.reshape(tp_count, own_count, proj_width + 128))
    own_sum = jnp.sum(gathered, axis=0)
    square_sum = own_sum[:, proj_width]
    own_qkv = (
        own_sum[:, :proj_width] * lax.rsqrt(square_sum / model_width + 1e-05)[:, None]
    ).astype(jnp.bfloat16)
    own_queries = own_qkv[:, :model_width]
    lanes = own_count * model_width // 128
    query = spread(
        jnp.broadcast_to(own_queries.reshape(1, lanes, 128), (tp_count, lanes, 128))
    ).reshape(all_rows, model_width)
    own_tokens = own_qkv[:, model_width:]
    own_keys = own_tokens[:, :kv_width].reshape(own_count, KV_HEADS, HEAD)
    own_values = own_tokens[:, kv_width:].reshape(own_count, KV_HEADS, HEAD)

    scale = HEAD ** (-0.5)
    key_index = tp_rank * own_count + jnp.arange(own_count, dtype=jnp.int32)
    key_place = key_index % tree
    reached = tree_reach(parents).reshape(all_rows, tree)
    column_pick = (jnp.arange(tree, dtype=jnp.int32)[:, None] == key_place[None, :]).astype(
        jnp.float32
    )
    on_path = jnp.dot(reached, column_pick, precision=lax.Precision.HIGHEST) > 0.5
    tree_mask = on_path & (key_place < draft_counts[0])[None, :]

    query_heads = query.reshape(all_rows, KV_HEADS, groups, HEAD)
    tree_scores = (
        jnp.einsum("tkgd,ukd->tkgu", query_heads, own_keys, preferred_element_type=jnp.float32)
        * scale
    )
    tree_scores = jnp.where(tree_mask[:, None, None, :], tree_scores, NEGATIVE)
    limit = (cache_lengths[:1] - tp_rank * places_dev).astype(jnp.int32)
    head_rows = jnp.transpose(query_heads, (1, 2, 0, 3)).reshape(KV_HEADS, groups * all_rows, HEAD)
    head_tree = jnp.transpose(tree_scores[..., 0], (1, 2, 0)).reshape(KV_HEADS, 1, groups * all_rows)
    cache_mixed, top_parts, total_parts = local_attention(
        limit, head_rows, cache_keys[0], cache_values[0], head_tree
    )
    shift = jnp.where(top_parts > 0.5 * NEGATIVE, top_parts, 0.0)
    tree_weight = lax.reduce_precision(jnp.exp(head_tree - shift), exponent_bits=8, mantissa_bits=7)
    head_mixed = cache_mixed + jnp.swapaxes(tree_weight, 1, 2) * own_values[0].reshape(
        KV_HEADS, 1, HEAD
    ).astype(jnp.float32)
    local_top = top_parts.reshape(HEADS, all_rows)
    totals = total_parts.reshape(HEADS, all_rows)

    columns = w_out.shape[0]
    per_head = HEAD // columns
    halves = HEAD // columns
    owner_mixed = jnp.swapaxes(
        head_mixed.reshape(HEADS, all_rows, halves, columns), 1, 2
    ).reshape(tp_count, all_rows * columns)
    owner_top = jnp.repeat(local_top, per_head, 0)
    owner_totals = jnp.repeat(totals, per_head, 0)
    packed = jnp.concatenate(
        [owner_mixed.astype(jnp.bfloat16)]
        + split3(owner_top)
        + split3(owner_totals)
        + [jnp.zeros((tp_count, 128 - (6 * all_rows) % 128), jnp.bfloat16)],
        axis=1,
    )
    got = spread(packed.reshape(tp_count, -1, 128)).reshape(tp_count, -1)
    flat = all_rows * columns
    piece = [got[:, flat + i * all_rows : flat + (i + 1) * all_rows] for i in range(6)]
    source_top = join3(*piece[:3])
    top = jnp.max(source_top, axis=0)
    rescale = jnp.exp(source_top - top[None])
    total = jnp.sum(rescale * join3(*piece[3:]), axis=0)
    source_mixed = got[:, :flat].reshape(tp_count, all_rows, columns).astype(jnp.float32)
    mixed_cols = jnp.sum(rescale[..., None] * source_mixed, axis=0)
    attended = (mixed_cols / total[:, None]).astype(jnp.bfloat16)

    partial_terms = jnp.dot(attended, w_out, preferred_element_type=jnp.float32)
    out_cols = model_width // tp_count
    owner_terms = jnp.swapaxes(partial_terms.reshape(all_rows, tp_count, out_cols), 0, 1)
    terms = spread(
        owner_terms.reshape(tp_count, all_rows * out_cols // 128, 128).astype(jnp.bfloat16)
    )
    projected = jnp.sum(terms.astype(jnp.float32), axis=0).reshape(all_rows, out_cols)
    return (inputs + projected).astype(jnp.bfloat16)


def solution(mesh):
    placed = (
        P("req", "tp"),
        P("tp"),
        P("tp", None),
        P("tp", None),
        P("req", "tp", None),
        P("req", "tp", None),
        P("req", None),
        P("req"),
        P("req"),
    )
    return jax.shard_map(
        on_device, mesh=mesh, in_specs=placed, out_specs=P("req", "tp"), check_vma=False
    )
```

```python
import jax
import jax.numpy as jnp
from jax import lax
from jax.experimental import pallas as pl
from jax.experimental.pallas import tpu as pltpu
from jax.sharding import PartitionSpec as P

HEADS = 32
KV_HEADS = 4
HEAD = 128


NEGATIVE = -1e30


def tree_reach(parents):
    width = parents.shape[1]
    places = jnp.arange(width, dtype=jnp.int32)
    parent_link = (parents[:, :, None] == places[None, None, :]).astype(jnp.float32)
    identity = (places[:, None] == places[None, :]).astype(jnp.float32)
    reached = jnp.minimum(parent_link + identity[None], 1.0)
    for rounds in range(width.bit_length()):
        reached = jnp.minimum(
            jnp.einsum("rij,rjk->rik", reached, reached, precision=lax.Precision.HIGHEST), 1.0
        )
    return reached


def attention_kernel(limit_ref, q_ref, k_ref, v_ref, tk_ref, tb_ref, o_ref, m_ref, l_ref, w_ref):
    rows, places = q_ref.shape[1], k_ref.shape[0]
    scale = HEAD ** (-0.5)
    query = q_ref[0]
    scores = (
        lax.dot_general(
            k_ref[...], query, (((1,), (1,)), ((), ())), preferred_element_type=jnp.float32
        )
        * scale
    )
    valid = lax.broadcasted_iota(jnp.int32, (places, rows), 0) < limit_ref[0]
    scores = jnp.where(valid, scores, NEGATIVE)
    own_scores = lax.dot_general(
        tk_ref[0], query, (((1,), (1,)), ((), ())), preferred_element_type=jnp.float32
    )
    tree_score = jnp.where(tb_ref[0] > 0.5, own_scores[0:1, :] * scale, NEGATIVE)
    top = jnp.maximum(jnp.max(scores, axis=0, keepdims=True), tree_score)
    shift = jnp.where(top > 0.5 * NEGATIVE, top, 0.0)
    weights = jnp.exp(scores - shift)
    tree_weight = jnp.exp(tree_score - shift)
    m_ref[0] = top
    l_ref[0] = jnp.sum(weights, axis=0, keepdims=True) + tree_weight
    w_ref[0] = tree_weight.astype(jnp.bfloat16).astype(jnp.float32)
    o_ref[0] = lax.dot_general(
        weights.astype(jnp.bfloat16),
        v_ref[...],
        (((0,), (0,)), ((), ())),
        preferred_element_type=jnp.float32,
    )


def local_attention(limit, query, keys, values, tree_keys, tree_valid):
    rows = query.shape[1]
    places = keys.shape[0]
    lane_row = pl.BlockSpec((1, 1, rows), lambda k, lim: (k, 0, 0))
    return pl.pallas_call(
        attention_kernel,
        grid_spec=pltpu.PrefetchScalarGridSpec(
            num_scalar_prefetch=1,
            grid=(KV_HEADS,),
            in_specs=[
                pl.BlockSpec((1, rows, HEAD), lambda k, lim: (k, 0, 0)),
                pl.BlockSpec((places, HEAD), lambda k, lim: (0, k)),
                pl.BlockSpec((places, HEAD), lambda k, lim: (0, k)),
                pl.BlockSpec((1, 8, HEAD), lambda k, lim: (k, 0, 0)),
                lane_row,
            ],
            out_specs=[
                pl.BlockSpec((1, rows, HEAD), lambda k, lim: (k, 0, 0)),
                lane_row,
                lane_row,
                lane_row,
            ],
        ),
        out_shape=[jax.ShapeDtypeStruct((KV_HEADS, rows, HEAD), jnp.float32)]
        + [jax.ShapeDtypeStruct((KV_HEADS, 1, rows), jnp.float32)] * 3,
    )(limit, query, keys, values, tree_keys, tree_valid)


def split3(values):
    high = lax.reduce_precision(values, exponent_bits=8, mantissa_bits=7)
    rest = values - high
    middle = lax.reduce_precision(rest, exponent_bits=8, mantissa_bits=7)
    low = rest - middle
    return [high.astype(jnp.bfloat16), middle.astype(jnp.bfloat16), low.astype(jnp.bfloat16)]


def join3(high, middle, low):
    return high.astype(jnp.float32) + middle.astype(jnp.float32) + low.astype(jnp.float32)


def spread(pieces):
    return lax.all_to_all(pieces, "tp", 0, 0, tiled=True)


def on_device(
    hidden, norm_gain, w_qkv, w_out, cache_keys, cache_values, parents, draft_counts, cache_lengths
):
    tp_count = lax.axis_size("tp")
    tp_rank = lax.axis_index("tp")
    model_width = w_out.shape[1]
    kv_width = KV_HEADS * HEAD
    groups = HEADS // KV_HEADS
    tree = parents.shape[1]
    places_dev = cache_keys.shape[1]
    inputs = hidden.astype(jnp.float32)
    all_rows = inputs.shape[0]
    own_count = all_rows // tp_count
    proj_width = w_qkv.shape[1]

    scaled = (inputs * norm_gain.astype(jnp.float32)[None, :]).astype(jnp.bfloat16)
    local_squares = jnp.sum(inputs * inputs, axis=1)
    partial = jnp.dot(scaled, w_qkv, preferred_element_type=jnp.float32)
    extended = jnp.concatenate(
        [partial, jnp.broadcast_to(local_squares[:, None], (all_rows, 128))], axis=1
    )
    gathered = spread(extended.reshape(tp_count, own_count, proj_width + 128))
    own_sum = jnp.sum(gathered, axis=0)
    square_sum = own_sum[:, proj_width]
    own_qkv = (
        own_sum[:, :proj_width] * lax.rsqrt(square_sum / model_width + 1e-05)[:, None]
    ).astype(jnp.bfloat16)
    own_queries = own_qkv[:, :model_width]
    lanes = own_count * model_width // 128
    query = spread(
        jnp.broadcast_to(own_queries.reshape(1, lanes, 128), (tp_count, lanes, 128))
    ).reshape(all_rows, model_width)
    own_tokens = own_qkv[:, model_width:]
    own_keys = own_tokens[:, :kv_width].reshape(own_count, KV_HEADS, HEAD)
    own_values = own_tokens[:, kv_width:].reshape(own_count, KV_HEADS, HEAD)

    scale = HEAD ** (-0.5)
    key_index = tp_rank * own_count + jnp.arange(own_count, dtype=jnp.int32)
    key_place = key_index % tree
    reached = tree_reach(parents).reshape(all_rows, tree)
    column_pick = (jnp.arange(tree, dtype=jnp.int32)[:, None] == key_place[None, :]).astype(
        jnp.float32
    )
    on_path = jnp.dot(reached, column_pick, precision=lax.Precision.HIGHEST) > 0.5
    tree_mask = on_path & (key_place < draft_counts[0])[None, :]

    query_heads = query.reshape(all_rows, KV_HEADS, groups, HEAD)
    limit = (cache_lengths[:1] - tp_rank * places_dev).astype(jnp.int32)
    head_rows = jnp.transpose(query_heads, (1, 2, 0, 3)).reshape(KV_HEADS, groups * all_rows, HEAD)
    tree_valid = jnp.broadcast_to(
        tree_mask[:, 0].astype(jnp.float32)[None, None, None, :], (KV_HEADS, 1, groups, all_rows)
    ).reshape(KV_HEADS, 1, groups * all_rows)
    cache_mixed, top_parts, total_parts, tree_weight = local_attention(
        limit,
        head_rows,
        cache_keys[0],
        cache_values[0],
        jnp.broadcast_to(own_keys[0][:, None, :], (KV_HEADS, 8, HEAD)),
        tree_valid,
    )
    head_mixed = cache_mixed + jnp.swapaxes(tree_weight, 1, 2) * own_values[0].reshape(
        KV_HEADS, 1, HEAD
    ).astype(jnp.float32)
    local_top = top_parts.reshape(HEADS, all_rows)
    totals = total_parts.reshape(HEADS, all_rows)

    columns = w_out.shape[0]
    per_head = HEAD // columns
    halves = HEAD // columns
    owner_mixed = jnp.swapaxes(
        head_mixed.reshape(HEADS, all_rows, halves, columns), 1, 2
    ).reshape(tp_count, all_rows * columns)
    owner_top = jnp.repeat(local_top, per_head, 0)
    owner_totals = jnp.repeat(totals, per_head, 0)
    packed = jnp.concatenate(
        [owner_mixed.astype(jnp.bfloat16)]
        + split3(owner_top)
        + split3(owner_totals)
        + [jnp.zeros((tp_count, 128 - (6 * all_rows) % 128), jnp.bfloat16)],
        axis=1,
    )
    got = spread(packed.reshape(tp_count, -1, 128)).reshape(tp_count, -1)
    flat = all_rows * columns
    piece = [got[:, flat + i * all_rows : flat + (i + 1) * all_rows] for i in range(6)]
    source_top = join3(*piece[:3])
    top = jnp.max(source_top, axis=0)
    rescale = jnp.exp(source_top - top[None])
    total = jnp.sum(rescale * join3(*piece[3:]), axis=0)
    source_mixed = got[:, :flat].reshape(tp_count, all_rows, columns).astype(jnp.float32)
    mixed_cols = jnp.sum(rescale[..., None] * source_mixed, axis=0)
    attended = (mixed_cols / total[:, None]).astype(jnp.bfloat16)

    partial_terms = jnp.dot(attended, w_out, preferred_element_type=jnp.float32)
    out_cols = model_width // tp_count
    owner_terms = jnp.swapaxes(partial_terms.reshape(all_rows, tp_count, out_cols), 0, 1)
    terms = spread(
        owner_terms.reshape(tp_count, all_rows * out_cols // 128, 128).astype(jnp.bfloat16)
    )
    projected = jnp.sum(terms.astype(jnp.float32), axis=0).reshape(all_rows, out_cols)
    return (inputs + projected).astype(jnp.bfloat16)


def solution(mesh):
    placed = (
        P("req", "tp"),
        P("tp"),
        P("tp", None),
        P("tp", None),
        P("req", "tp", None),
        P("req", "tp", None),
        P("req", None),
        P("req"),
        P("req"),
    )
    return jax.shard_map(
        on_device, mesh=mesh, in_specs=placed, out_specs=P("req", "tp"), check_vma=False
    )
```

```python
import jax
import jax.numpy as jnp
from jax import lax
from jax.experimental import pallas as pl
from jax.experimental.pallas import tpu as pltpu
from jax.sharding import PartitionSpec as P

HEADS = 32
KV_HEADS = 4
HEAD = 128


NEGATIVE = -1e30


def tree_reach(parents):
    width = parents.shape[1]
    places = jnp.arange(width, dtype=jnp.int32)
    parent_link = (parents[:, :, None] == places[None, None, :]).astype(jnp.float32)
    identity = (places[:, None] == places[None, :]).astype(jnp.float32)
    reached = jnp.minimum(parent_link + identity[None], 1.0)
    for rounds in range(width.bit_length()):
        reached = jnp.minimum(
            jnp.einsum("rij,rjk->rik", reached, reached, precision=lax.Precision.HIGHEST), 1.0
        )
    return reached


def attention_kernel(limit_ref, q_ref, k_ref, v_ref, tk_ref, tb_ref, o_ref, m_ref, l_ref, w_ref):
    rows, places = q_ref.shape[1], k_ref.shape[0]
    scale = HEAD ** (-0.5)
    query = q_ref[0]
    scores = (
        lax.dot_general(
            k_ref[...], query, (((1,), (1,)), ((), ())), preferred_element_type=jnp.float32
        )
        * scale
    )
    position = lax.broadcasted_iota(jnp.int32, (places, 1), 0)
    scores = scores + jnp.where(position < limit_ref[0], 0.0, NEGATIVE)
    own_scores = lax.dot_general(
        tk_ref[0], query, (((1,), (1,)), ((), ())), preferred_element_type=jnp.float32
    )
    tree_score = jnp.where(tb_ref[0] > 0.5, own_scores[0:1, :] * scale, NEGATIVE)
    top = jnp.maximum(jnp.max(scores, axis=0, keepdims=True), tree_score)
    shift = jnp.where(top > 0.5 * NEGATIVE, top, 0.0)
    weights = jnp.exp(scores - shift)
    tree_weight = jnp.exp(tree_score - shift)
    m_ref[0] = top
    l_ref[0] = jnp.sum(weights, axis=0, keepdims=True) + tree_weight
    w_ref[0] = tree_weight.astype(jnp.bfloat16).astype(jnp.float32)
    o_ref[0] = lax.dot_general(
        weights.astype(jnp.bfloat16),
        v_ref[...],
        (((0,), (0,)), ((), ())),
        preferred_element_type=jnp.float32,
    )


def local_attention(limit, query, keys, values, tree_keys, tree_valid):
    rows = query.shape[1]
    places = keys.shape[0]
    lane_row = pl.BlockSpec((1, 1, rows), lambda k, lim: (k, 0, 0))
    return pl.pallas_call(
        attention_kernel,
        grid_spec=pltpu.PrefetchScalarGridSpec(
            num_scalar_prefetch=1,
            grid=(KV_HEADS,),
            in_specs=[
                pl.BlockSpec((1, rows, HEAD), lambda k, lim: (k, 0, 0)),
                pl.BlockSpec((places, HEAD), lambda k, lim: (0, k)),
                pl.BlockSpec((places, HEAD), lambda k, lim: (0, k)),
                pl.BlockSpec((1, 8, HEAD), lambda k, lim: (k, 0, 0)),
                lane_row,
            ],
            out_specs=[
                pl.BlockSpec((1, rows, HEAD), lambda k, lim: (k, 0, 0)),
                lane_row,
                lane_row,
                lane_row,
            ],
        ),
        out_shape=[jax.ShapeDtypeStruct((KV_HEADS, rows, HEAD), jnp.float32)]
        + [jax.ShapeDtypeStruct((KV_HEADS, 1, rows), jnp.float32)] * 3,
    )(limit, query, keys, values, tree_keys, tree_valid)


def split3(values):
    high = lax.reduce_precision(values, exponent_bits=8, mantissa_bits=7)
    rest = values - high
    middle = lax.reduce_precision(rest, exponent_bits=8, mantissa_bits=7)
    low = rest - middle
    return [high.astype(jnp.bfloat16), middle.astype(jnp.bfloat16), low.astype(jnp.bfloat16)]


def join3(high, middle, low):
    return high.astype(jnp.float32) + middle.astype(jnp.float32) + low.astype(jnp.float32)


def spread(pieces):
    return lax.all_to_all(pieces, "tp", 0, 0, tiled=True)


def on_device(
    hidden, norm_gain, w_qkv, w_out, cache_keys, cache_values, parents, draft_counts, cache_lengths
):
    tp_count = lax.axis_size("tp")
    tp_rank = lax.axis_index("tp")
    model_width = w_out.shape[1]
    kv_width = KV_HEADS * HEAD
    groups = HEADS // KV_HEADS
    tree = parents.shape[1]
    places_dev = cache_keys.shape[1]
    inputs = hidden.astype(jnp.float32)
    all_rows = inputs.shape[0]
    own_count = all_rows // tp_count
    proj_width = w_qkv.shape[1]

    scaled = (inputs * norm_gain.astype(jnp.float32)[None, :]).astype(jnp.bfloat16)
    local_squares = jnp.sum(inputs * inputs, axis=1)
    partial = jnp.dot(scaled, w_qkv, preferred_element_type=jnp.float32)
    extended = jnp.concatenate(
        [partial, jnp.broadcast_to(local_squares[:, None], (all_rows, 128))], axis=1
    )
    gathered = spread(extended.reshape(tp_count, own_count, proj_width + 128))
    own_sum = jnp.sum(gathered, axis=0)
    square_sum = own_sum[:, proj_width]
    own_qkv = (
        own_sum[:, :proj_width] * lax.rsqrt(square_sum / model_width + 1e-05)[:, None]
    ).astype(jnp.bfloat16)
    own_queries = own_qkv[:, :model_width]
    lanes = own_count * model_width // 128
    query = spread(
        jnp.broadcast_to(own_queries.reshape(1, lanes, 128), (tp_count, lanes, 128))
    ).reshape(all_rows, model_width)
    own_tokens = own_qkv[:, model_width:]
    own_keys = own_tokens[:, :kv_width].reshape(own_count, KV_HEADS, HEAD)
    own_values = own_tokens[:, kv_width:].reshape(own_count, KV_HEADS, HEAD)

    scale = HEAD ** (-0.5)
    key_index = tp_rank * own_count + jnp.arange(own_count, dtype=jnp.int32)
    key_place = key_index % tree
    reached = tree_reach(parents).reshape(all_rows, tree)
    column_pick = (jnp.arange(tree, dtype=jnp.int32)[:, None] == key_place[None, :]).astype(
        jnp.float32
    )
    on_path = jnp.dot(reached, column_pick, precision=lax.Precision.HIGHEST) > 0.5
    tree_mask = on_path & (key_place < draft_counts[0])[None, :]

    query_heads = query.reshape(all_rows, KV_HEADS, groups, HEAD)
    limit = (cache_lengths[:1] - tp_rank * places_dev).astype(jnp.int32)
    head_rows = jnp.transpose(query_heads, (1, 2, 0, 3)).reshape(KV_HEADS, groups * all_rows, HEAD)
    tree_valid = jnp.broadcast_to(
        tree_mask[:, 0].astype(jnp.float32)[None, None, None, :], (KV_HEADS, 1, groups, all_rows)
    ).reshape(KV_HEADS, 1, groups * all_rows)
    cache_mixed, top_parts, total_parts, tree_weight = local_attention(
        limit,
        head_rows,
        cache_keys[0],
        cache_values[0],
        jnp.broadcast_to(own_keys[0][:, None, :], (KV_HEADS, 8, HEAD)),
        tree_valid,
    )
    head_mixed = cache_mixed + jnp.swapaxes(tree_weight, 1, 2) * own_values[0].reshape(
        KV_HEADS, 1, HEAD
    ).astype(jnp.float32)
    local_top = top_parts.reshape(HEADS, all_rows)
    totals = total_parts.reshape(HEADS, all_rows)

    columns = w_out.shape[0]
    per_head = HEAD // columns
    halves = HEAD // columns
    owner_mixed = jnp.swapaxes(
        head_mixed.reshape(HEADS, all_rows, halves, columns), 1, 2
    ).reshape(tp_count, all_rows * columns)
    owner_top = jnp.repeat(local_top, per_head, 0)
    owner_totals = jnp.repeat(totals, per_head, 0)
    packed = jnp.concatenate(
        [owner_mixed.astype(jnp.bfloat16)]
        + split3(owner_top)
        + split3(owner_totals)
        + [jnp.zeros((tp_count, 128 - (6 * all_rows) % 128), jnp.bfloat16)],
        axis=1,
    )
    got = spread(packed.reshape(tp_count, -1, 128)).reshape(tp_count, -1)
    flat = all_rows * columns
    piece = [got[:, flat + i * all_rows : flat + (i + 1) * all_rows] for i in range(6)]
    source_top = join3(*piece[:3])
    top = jnp.max(source_top, axis=0)
    rescale = jnp.exp(source_top - top[None])
    total = jnp.sum(rescale * join3(*piece[3:]), axis=0)
    source_mixed = got[:, :flat].reshape(tp_count, all_rows, columns).astype(jnp.float32)
    mixed_cols = jnp.sum(rescale[..., None] * source_mixed, axis=0)
    attended = (mixed_cols / total[:, None]).astype(jnp.bfloat16)

    partial_terms = jnp.dot(attended, w_out, preferred_element_type=jnp.float32)
    out_cols = model_width // tp_count
    owner_terms = jnp.swapaxes(partial_terms.reshape(all_rows, tp_count, out_cols), 0, 1)
    terms = spread(
        owner_terms.reshape(tp_count, all_rows * out_cols // 128, 128).astype(jnp.bfloat16)
    )
    projected = jnp.sum(terms.astype(jnp.float32), axis=0).reshape(all_rows, out_cols)
    return (inputs + projected).astype(jnp.bfloat16)


def solution(mesh):
    placed = (
        P("req", "tp"),
        P("tp"),
        P("tp", None),
        P("tp", None),
        P("req", "tp", None),
        P("req", "tp", None),
        P("req", None),
        P("req"),
        P("req"),
    )
    return jax.shard_map(
        on_device, mesh=mesh, in_specs=placed, out_specs=P("req", "tp"), check_vma=False
    )
```

```python
import jax
import jax.numpy as jnp
from jax import lax
from jax.experimental import pallas as pl
from jax.experimental.pallas import tpu as pltpu
from jax.sharding import PartitionSpec as P

HEADS = 32
KV_HEADS = 4
HEAD = 128


NEGATIVE = -1e30


def tree_reach(parents):
    width = parents.shape[1]
    places = jnp.arange(width, dtype=jnp.int32)
    parent_link = (parents[:, :, None] == places[None, None, :]).astype(jnp.float32)
    identity = (places[:, None] == places[None, :]).astype(jnp.float32)
    reached = jnp.minimum(parent_link + identity[None], 1.0)
    for rounds in range(width.bit_length()):
        reached = jnp.minimum(
            jnp.einsum("rij,rjk->rik", reached, reached, precision=lax.Precision.HIGHEST), 1.0
        )
    return reached


def attention_kernel(limit_ref, q_ref, k_ref, v_ref, tk_ref, tb_ref, o_ref, m_ref, l_ref, w_ref):
    rows, places = q_ref.shape[1], k_ref.shape[0]
    scale = HEAD ** (-0.5)
    query = q_ref[0]
    scores = (
        lax.dot_general(
            k_ref[...], query, (((1,), (1,)), ((), ())), preferred_element_type=jnp.float32
        )
        * scale
    )
    position = lax.broadcasted_iota(jnp.int32, (places, 1), 0)
    scores = scores + jnp.where(position < limit_ref[0], 0.0, NEGATIVE)
    own_scores = lax.dot_general(
        tk_ref[0], query, (((1,), (1,)), ((), ())), preferred_element_type=jnp.float32
    )
    tree_score = jnp.where(tb_ref[0] > 0.5, own_scores[0:1, :] * scale, NEGATIVE)
    top = jnp.maximum(jnp.max(scores, axis=0, keepdims=True), tree_score)
    shift = jnp.where(top > 0.5 * NEGATIVE, top, 0.0)
    weights = jnp.exp(scores - shift)
    tree_weight = jnp.exp(tree_score - shift)
    m_ref[0] = top
    l_ref[0] = jnp.sum(weights, axis=0, keepdims=True) + tree_weight
    w_ref[0] = tree_weight.astype(jnp.bfloat16).astype(jnp.float32)
    o_ref[0] = lax.dot_general(
        weights.astype(jnp.bfloat16),
        v_ref[...],
        (((0,), (0,)), ((), ())),
        preferred_element_type=jnp.float32,
    )


def local_attention(limit, query, keys, values, tree_keys, tree_valid):
    rows = query.shape[1]
    places = keys.shape[0]
    lane_row = pl.BlockSpec((1, 1, rows), lambda k, lim: (k, 0, 0))
    return pl.pallas_call(
        attention_kernel,
        grid_spec=pltpu.PrefetchScalarGridSpec(
            num_scalar_prefetch=1,
            grid=(KV_HEADS,),
            in_specs=[
                pl.BlockSpec((1, rows, HEAD), lambda k, lim: (k, 0, 0)),
                pl.BlockSpec((places, HEAD), lambda k, lim: (0, k)),
                pl.BlockSpec((places, HEAD), lambda k, lim: (0, k)),
                pl.BlockSpec((1, 8, HEAD), lambda k, lim: (k, 0, 0)),
                lane_row,
            ],
            out_specs=[
                pl.BlockSpec((1, rows, HEAD), lambda k, lim: (k, 0, 0)),
                lane_row,
                lane_row,
                lane_row,
            ],
        ),
        out_shape=[jax.ShapeDtypeStruct((KV_HEADS, rows, HEAD), jnp.float32)]
        + [jax.ShapeDtypeStruct((KV_HEADS, 1, rows), jnp.float32)] * 3,
    )(limit, query, keys, values, tree_keys, tree_valid)


def split3(values):
    high = lax.reduce_precision(values, exponent_bits=8, mantissa_bits=7)
    rest = values - high
    middle = lax.reduce_precision(rest, exponent_bits=8, mantissa_bits=7)
    low = rest - middle
    return [high.astype(jnp.bfloat16), middle.astype(jnp.bfloat16), low.astype(jnp.bfloat16)]


def join3(high, middle, low):
    return high.astype(jnp.float32) + middle.astype(jnp.float32) + low.astype(jnp.float32)


def spread(pieces):
    return lax.all_to_all(pieces, "tp", 0, 0, tiled=True)


def on_device(
    hidden, norm_gain, w_qkv, w_out, cache_keys, cache_values, parents, draft_counts, cache_lengths
):
    tp_count = lax.axis_size("tp")
    tp_rank = lax.axis_index("tp")
    model_width = w_out.shape[1]
    kv_width = KV_HEADS * HEAD
    groups = HEADS // KV_HEADS
    tree = parents.shape[1]
    places_dev = cache_keys.shape[1]
    inputs = hidden.astype(jnp.float32)
    all_rows = inputs.shape[0]
    own_count = all_rows // tp_count
    proj_width = w_qkv.shape[1]

    scaled = (inputs * norm_gain.astype(jnp.float32)[None, :]).astype(jnp.bfloat16)
    local_squares = jnp.sum(inputs * inputs, axis=1)
    partial = jnp.dot(scaled, w_qkv, preferred_element_type=jnp.float32)
    extended = jnp.concatenate(
        [partial, jnp.broadcast_to(local_squares[:, None], (all_rows, 128))], axis=1
    )
    gathered = spread(extended.reshape(tp_count, own_count, proj_width + 128))
    own_sum = jnp.sum(gathered, axis=0)
    square_sum = own_sum[:, proj_width]
    own_qkv = (
        own_sum[:, :proj_width] * lax.rsqrt(square_sum / model_width + 1e-05)[:, None]
    ).astype(jnp.bfloat16)
    own_queries = own_qkv[:, :model_width]
    lanes = own_count * model_width // 128
    query = spread(
        jnp.broadcast_to(own_queries.reshape(1, lanes, 128), (tp_count, lanes, 128))
    ).reshape(all_rows, model_width)
    own_tokens = own_qkv[:, model_width:]
    own_keys = own_tokens[:, :kv_width].reshape(own_count, KV_HEADS, HEAD)
    own_values = own_tokens[:, kv_width:].reshape(own_count, KV_HEADS, HEAD)

    scale = HEAD ** (-0.5)
    key_index = tp_rank * own_count + jnp.arange(own_count, dtype=jnp.int32)
    key_place = key_index % tree
    reached = tree_reach(parents).reshape(all_rows, tree)
    column_pick = (jnp.arange(tree, dtype=jnp.int32)[:, None] == key_place[None, :]).astype(
        jnp.float32
    )
    on_path = jnp.dot(reached, column_pick, precision=lax.Precision.HIGHEST) > 0.5
    tree_mask = on_path & (key_place < draft_counts[0])[None, :]

    query_heads = query.reshape(all_rows, KV_HEADS, groups, HEAD)
    limit = (cache_lengths[:1] - tp_rank * places_dev).astype(jnp.int32)
    head_rows = jnp.transpose(query_heads, (1, 2, 0, 3)).reshape(KV_HEADS, groups * all_rows, HEAD)
    tree_valid = jnp.broadcast_to(
        tree_mask[:, 0].astype(jnp.float32)[None, None, None, :], (KV_HEADS, 1, groups, all_rows)
    ).reshape(KV_HEADS, 1, groups * all_rows)
    cache_mixed, top_parts, total_parts, tree_weight = local_attention(
        limit,
        head_rows,
        cache_keys[0],
        cache_values[0],
        jnp.broadcast_to(own_keys[0][:, None, :], (KV_HEADS, 8, HEAD)),
        tree_valid,
    )
    head_mixed = cache_mixed + jnp.swapaxes(tree_weight, 1, 2) * own_values[0].reshape(
        KV_HEADS, 1, HEAD
    ).astype(jnp.float32)
    local_top = top_parts.reshape(HEADS, all_rows)
    totals = total_parts.reshape(HEADS, all_rows)

    columns = w_out.shape[0]
    per_head = HEAD // columns
    halves = HEAD // columns
    owner_mixed = jnp.swapaxes(
        head_mixed.reshape(HEADS, all_rows, halves, columns), 1, 2
    ).reshape(tp_count, all_rows * columns)
    owner_top = jnp.repeat(local_top, per_head, 0)
    owner_totals = jnp.repeat(totals, per_head, 0)
    packed = jnp.concatenate(
        [owner_mixed.astype(jnp.bfloat16)]
        + split3(owner_top)
        + split3(owner_totals)
        + [jnp.zeros((tp_count, 128 - (6 * all_rows) % 128), jnp.bfloat16)],
        axis=1,
    )
    got = spread(packed.reshape(tp_count, -1, 128)).reshape(tp_count, -1)
    flat = all_rows * columns
    piece = [got[:, flat + i * all_rows : flat + (i + 1) * all_rows] for i in range(6)]
    source_top = join3(*piece[:3])
    top = jnp.max(source_top, axis=0)
    rescale = jnp.exp(source_top - top[None])
    total = jnp.sum(rescale * join3(*piece[3:]), axis=0)
    source_mixed = got[:, :flat].reshape(tp_count, all_rows, columns).astype(jnp.float32)
    mixed_cols = jnp.einsum(
        "st,stc->tc", rescale, source_mixed, precision=lax.Precision.HIGHEST
    )
    attended = (mixed_cols / total[:, None]).astype(jnp.bfloat16)

    partial_terms = jnp.dot(attended, w_out, preferred_element_type=jnp.float32)
    out_cols = model_width // tp_count
    owner_terms = jnp.swapaxes(partial_terms.reshape(all_rows, tp_count, out_cols), 0, 1)
    terms = spread(
        owner_terms.reshape(tp_count, all_rows * out_cols // 128, 128).astype(jnp.bfloat16)
    )
    projected = jnp.sum(terms.astype(jnp.float32), axis=0).reshape(all_rows, out_cols)
    return (inputs + projected).astype(jnp.bfloat16)


def solution(mesh):
    placed = (
        P("req", "tp"),
        P("tp"),
        P("tp", None),
        P("tp", None),
        P("req", "tp", None),
        P("req", "tp", None),
        P("req", None),
        P("req"),
        P("req"),
    )
    return jax.shard_map(
        on_device, mesh=mesh, in_specs=placed, out_specs=P("req", "tp"), check_vma=False
    )
```

```python
import jax
import jax.numpy as jnp
from jax import lax
from jax.experimental import pallas as pl
from jax.experimental.pallas import tpu as pltpu
from jax.sharding import Mesh
from jax.sharding import PartitionSpec as P

HEADS = 32
KV_HEADS = 4
HEAD = 128
TP = ("z", "y", "c")
CHIP = ("z", "y")


NEGATIVE = -1e30


def tree_reach(parents):
    width = parents.shape[1]
    places = jnp.arange(width, dtype=jnp.int32)
    parent_link = (parents[:, :, None] == places[None, None, :]).astype(jnp.float32)
    identity = (places[:, None] == places[None, :]).astype(jnp.float32)
    reached = jnp.minimum(parent_link + identity[None], 1.0)
    for rounds in range(width.bit_length()):
        reached = jnp.minimum(
            jnp.einsum("rij,rjk->rik", reached, reached, precision=lax.Precision.HIGHEST), 1.0
        )
    return reached


def attention_kernel(limit_ref, q_ref, k_ref, v_ref, tk_ref, tb_ref, o_ref, m_ref, l_ref, w_ref):
    rows, places = q_ref.shape[1], k_ref.shape[0]
    scale = HEAD ** (-0.5)
    query = q_ref[0]
    scores = (
        lax.dot_general(
            k_ref[...], query, (((1,), (1,)), ((), ())), preferred_element_type=jnp.float32
        )
        * scale
    )
    position = lax.broadcasted_iota(jnp.int32, (places, 1), 0)
    scores = scores + jnp.where(position < limit_ref[0], 0.0, NEGATIVE)
    own_scores = lax.dot_general(
        tk_ref[0], query, (((1,), (1,)), ((), ())), preferred_element_type=jnp.float32
    )
    tree_score = jnp.where(tb_ref[0] > 0.5, own_scores[0:1, :] * scale, NEGATIVE)
    top = jnp.maximum(jnp.max(scores, axis=0, keepdims=True), tree_score)
    shift = jnp.where(top > 0.5 * NEGATIVE, top, 0.0)
    weights = jnp.exp(scores - shift)
    tree_weight = jnp.exp(tree_score - shift)
    m_ref[0] = top
    l_ref[0] = jnp.sum(weights, axis=0, keepdims=True) + tree_weight
    w_ref[0] = tree_weight.astype(jnp.bfloat16).astype(jnp.float32)
    o_ref[0] = lax.dot_general(
        weights.astype(jnp.bfloat16),
        v_ref[...],
        (((0,), (0,)), ((), ())),
        preferred_element_type=jnp.float32,
    )


def local_attention(limit, query, keys, values, tree_keys, tree_valid):
    rows = query.shape[1]
    places = keys.shape[0]
    lane_row = pl.BlockSpec((1, 1, rows), lambda k, lim: (k, 0, 0))
    return pl.pallas_call(
        attention_kernel,
        grid_spec=pltpu.PrefetchScalarGridSpec(
            num_scalar_prefetch=1,
            grid=(KV_HEADS,),
            in_specs=[
                pl.BlockSpec((1, rows, HEAD), lambda k, lim: (k, 0, 0)),
                pl.BlockSpec((places, HEAD), lambda k, lim: (0, k)),
                pl.BlockSpec((places, HEAD), lambda k, lim: (0, k)),
                pl.BlockSpec((1, 8, HEAD), lambda k, lim: (k, 0, 0)),
                lane_row,
            ],
            out_specs=[
                pl.BlockSpec((1, rows, HEAD), lambda k, lim: (k, 0, 0)),
                lane_row,
                lane_row,
                lane_row,
            ],
        ),
        out_shape=[jax.ShapeDtypeStruct((KV_HEADS, rows, HEAD), jnp.float32)]
        + [jax.ShapeDtypeStruct((KV_HEADS, 1, rows), jnp.float32)] * 3,
    )(limit, query, keys, values, tree_keys, tree_valid)


def split3(values):
    high = lax.reduce_precision(values, exponent_bits=8, mantissa_bits=7)
    rest = values - high
    middle = lax.reduce_precision(rest, exponent_bits=8, mantissa_bits=7)
    low = rest - middle
    return [high.astype(jnp.bfloat16), middle.astype(jnp.bfloat16), low.astype(jnp.bfloat16)]


def join3(high, middle, low):
    return high.astype(jnp.float32) + middle.astype(jnp.float32) + low.astype(jnp.float32)


def spread(pieces):
    return lax.all_to_all(pieces, TP, 0, 0, tiled=True)


def on_device(
    hidden, norm_gain, w_qkv, w_out, cache_keys, cache_values, parents, draft_counts, cache_lengths
):
    cores = lax.axis_size("c")
    tp_count = lax.axis_size(CHIP) * cores
    tp_rank = lax.axis_index(CHIP) * cores + lax.axis_index("c")
    model_width = w_out.shape[1]
    kv_width = KV_HEADS * HEAD
    groups = HEADS // KV_HEADS
    tree = parents.shape[1]
    places_dev = cache_keys.shape[1]
    inputs = hidden.astype(jnp.float32)
    all_rows = inputs.shape[0]
    own_count = all_rows // tp_count
    proj_width = w_qkv.shape[1]

    scaled = (inputs * norm_gain.astype(jnp.float32)[None, :]).astype(jnp.bfloat16)
    local_squares = jnp.sum(inputs * inputs, axis=1)
    partial = jnp.dot(scaled, w_qkv, preferred_element_type=jnp.float32)
    extended = jnp.concatenate(
        [partial, jnp.broadcast_to(local_squares[:, None], (all_rows, 128))], axis=1
    )
    by_core = extended.reshape(tp_count // cores, cores, own_count, proj_width + 128)
    chip_sum = jnp.sum(lax.all_to_all(by_core, "c", 1, 1, tiled=True), axis=1)
    gathered = lax.all_to_all(chip_sum, CHIP, 0, 0, tiled=True)
    own_sum = jnp.sum(gathered, axis=0)
    square_sum = own_sum[:, proj_width]
    own_qkv = (
        own_sum[:, :proj_width] * lax.rsqrt(square_sum / model_width + 1e-05)[:, None]
    ).astype(jnp.bfloat16)
    own_queries = own_qkv[:, :model_width]
    lanes = own_count * model_width // 128
    query = spread(
        jnp.broadcast_to(own_queries.reshape(1, lanes, 128), (tp_count, lanes, 128))
    ).reshape(all_rows, model_width)
    own_tokens = own_qkv[:, model_width:]
    own_keys = own_tokens[:, :kv_width].reshape(own_count, KV_HEADS, HEAD)
    own_values = own_tokens[:, kv_width:].reshape(own_count, KV_HEADS, HEAD)

    scale = HEAD ** (-0.5)
    key_index = tp_rank * own_count + jnp.arange(own_count, dtype=jnp.int32)
    key_place = key_index % tree
    reached = tree_reach(parents).reshape(all_rows, tree)
    column_pick = (jnp.arange(tree, dtype=jnp.int32)[:, None] == key_place[None, :]).astype(
        jnp.float32
    )
    on_path = jnp.dot(reached, column_pick, precision=lax.Precision.HIGHEST) > 0.5
    tree_mask = on_path & (key_place < draft_counts[0])[None, :]

    query_heads = query.reshape(all_rows, KV_HEADS, groups, HEAD)
    limit = (cache_lengths[:1] - tp_rank * places_dev).astype(jnp.int32)
    head_rows = jnp.transpose(query_heads, (1, 2, 0, 3)).reshape(KV_HEADS, groups * all_rows, HEAD)
    tree_valid = jnp.broadcast_to(
        tree_mask[:, 0].astype(jnp.float32)[None, None, None, :], (KV_HEADS, 1, groups, all_rows)
    ).reshape(KV_HEADS, 1, groups * all_rows)
    cache_mixed, top_parts, total_parts, tree_weight = local_attention(
        limit,
        head_rows,
        cache_keys[0],
        cache_values[0],
        jnp.broadcast_to(own_keys[0][:, None, :], (KV_HEADS, 8, HEAD)),
        tree_valid,
    )
    head_mixed = cache_mixed + jnp.swapaxes(tree_weight, 1, 2) * own_values[0].reshape(
        KV_HEADS, 1, HEAD
    ).astype(jnp.float32)
    local_top = top_parts.reshape(HEADS, all_rows)
    totals = total_parts.reshape(HEADS, all_rows)

    columns = w_out.shape[0]
    per_head = HEAD // columns
    halves = HEAD // columns
    owner_mixed = jnp.swapaxes(
        head_mixed.reshape(HEADS, all_rows, halves, columns), 1, 2
    ).reshape(tp_count, all_rows * columns)
    owner_top = jnp.repeat(local_top, per_head, 0)
    owner_totals = jnp.repeat(totals, per_head, 0)
    packed = jnp.concatenate(
        [owner_mixed.astype(jnp.bfloat16)]
        + split3(owner_top)
        + split3(owner_totals)
        + [jnp.zeros((tp_count, 128 - (6 * all_rows) % 128), jnp.bfloat16)],
        axis=1,
    )
    got = spread(packed.reshape(tp_count, -1, 128)).reshape(tp_count, -1)
    flat = all_rows * columns
    piece = [got[:, flat + i * all_rows : flat + (i + 1) * all_rows] for i in range(6)]
    source_top = join3(*piece[:3])
    top = jnp.max(source_top, axis=0)
    rescale = jnp.exp(source_top - top[None])
    total = jnp.sum(rescale * join3(*piece[3:]), axis=0)
    source_mixed = got[:, :flat].reshape(tp_count, all_rows, columns).astype(jnp.float32)
    mixed_cols = jnp.einsum(
        "st,stc->tc", rescale, source_mixed, precision=lax.Precision.HIGHEST
    )
    attended = (mixed_cols / total[:, None]).astype(jnp.bfloat16)

    partial_terms = jnp.dot(attended, w_out, preferred_element_type=jnp.float32)
    out_cols = model_width // tp_count
    owner_terms = jnp.swapaxes(partial_terms.reshape(all_rows, tp_count, out_cols), 0, 1)
    terms = spread(
        owner_terms.reshape(tp_count, all_rows * out_cols // 128, 128).astype(jnp.bfloat16)
    )
    projected = jnp.sum(terms.astype(jnp.float32), axis=0).reshape(all_rows, out_cols)
    return (inputs + projected).astype(jnp.bfloat16)


def solution(mesh):
    tp = mesh.shape["tp"]
    split = Mesh(mesh.devices.reshape(mesh.shape["req"], tp // 8, 4, 2), ("req",) + TP)
    placed = (
        P("req", TP),
        P(TP),
        P(TP, None),
        P(TP, None),
        P("req", TP, None),
        P("req", TP, None),
        P("req", None),
        P("req"),
        P("req"),
    )
    return jax.shard_map(
        on_device, mesh=split, in_specs=placed, out_specs=P("req", TP), check_vma=False
    )
```

```python
import jax
import jax.numpy as jnp
from jax import lax
from jax.experimental import pallas as pl
from jax.experimental.pallas import tpu as pltpu
from jax.sharding import Mesh
from jax.sharding import PartitionSpec as P

HEADS = 32
KV_HEADS = 4
HEAD = 128
TP = ("z", "y", "c")
CHIP = ("z", "y")


NEGATIVE = -1e30


def tree_reach(parents):
    width = parents.shape[1]
    places = jnp.arange(width, dtype=jnp.int32)
    parent_link = (parents[:, :, None] == places[None, None, :]).astype(jnp.float32)
    identity = (places[:, None] == places[None, :]).astype(jnp.float32)
    reached = jnp.minimum(parent_link + identity[None], 1.0)
    for rounds in range(width.bit_length()):
        reached = jnp.minimum(
            jnp.einsum("rij,rjk->rik", reached, reached, precision=lax.Precision.HIGHEST), 1.0
        )
    return reached


def attention_kernel(limit_ref, q_ref, k_ref, v_ref, tk_ref, tb_ref, o_ref, m_ref, l_ref, w_ref):
    rows, places = q_ref.shape[1], k_ref.shape[0]
    scale = HEAD ** (-0.5)
    query = q_ref[0]
    scores = (
        lax.dot_general(
            k_ref[...], query, (((1,), (1,)), ((), ())), preferred_element_type=jnp.float32
        )
        * scale
    )
    position = lax.broadcasted_iota(jnp.int32, (places, 1), 0)
    scores = scores + jnp.where(position < limit_ref[0], 0.0, NEGATIVE)
    own_scores = lax.dot_general(
        tk_ref[0], query, (((1,), (1,)), ((), ())), preferred_element_type=jnp.float32
    )
    tree_score = jnp.where(tb_ref[0] > 0.5, own_scores[0:1, :] * scale, NEGATIVE)
    top = jnp.maximum(jnp.max(scores, axis=0, keepdims=True), tree_score)
    shift = jnp.where(top > 0.5 * NEGATIVE, top, 0.0)
    weights = jnp.exp(scores - shift)
    tree_weight = jnp.exp(tree_score - shift)
    m_ref[0] = top
    l_ref[0] = jnp.sum(weights, axis=0, keepdims=True) + tree_weight
    w_ref[0] = tree_weight.astype(jnp.bfloat16).astype(jnp.float32)
    o_ref[0] = lax.dot_general(
        weights.astype(jnp.bfloat16),
        v_ref[...],
        (((0,), (0,)), ((), ())),
        preferred_element_type=jnp.float32,
    )


def local_attention(limit, query, keys, values, tree_keys, tree_valid):
    rows = query.shape[1]
    places = keys.shape[0]
    lane_row = pl.BlockSpec((1, 1, rows), lambda k, lim: (k, 0, 0))
    return pl.pallas_call(
        attention_kernel,
        grid_spec=pltpu.PrefetchScalarGridSpec(
            num_scalar_prefetch=1,
            grid=(KV_HEADS,),
            in_specs=[
                pl.BlockSpec((1, rows, HEAD), lambda k, lim: (k, 0, 0)),
                pl.BlockSpec((places, HEAD), lambda k, lim: (0, k)),
                pl.BlockSpec((places, HEAD), lambda k, lim: (0, k)),
                pl.BlockSpec((1, 8, HEAD), lambda k, lim: (k, 0, 0)),
                lane_row,
            ],
            out_specs=[
                pl.BlockSpec((1, rows, HEAD), lambda k, lim: (k, 0, 0)),
                lane_row,
                lane_row,
                lane_row,
            ],
        ),
        out_shape=[jax.ShapeDtypeStruct((KV_HEADS, rows, HEAD), jnp.float32)]
        + [jax.ShapeDtypeStruct((KV_HEADS, 1, rows), jnp.float32)] * 3,
    )(limit, query, keys, values, tree_keys, tree_valid)


def split3(values):
    high = lax.reduce_precision(values, exponent_bits=8, mantissa_bits=7)
    rest = values - high
    middle = lax.reduce_precision(rest, exponent_bits=8, mantissa_bits=7)
    low = rest - middle
    return [high.astype(jnp.bfloat16), middle.astype(jnp.bfloat16), low.astype(jnp.bfloat16)]


def join3(high, middle, low):
    return high.astype(jnp.float32) + middle.astype(jnp.float32) + low.astype(jnp.float32)


def spread(pieces):
    return lax.all_to_all(pieces, TP, 0, 0, tiled=True)


def on_device(
    hidden, norm_gain, w_qkv, w_out, cache_keys, cache_values, parents, draft_counts, cache_lengths
):
    cores = lax.axis_size("c")
    tp_count = lax.axis_size(CHIP) * cores
    tp_rank = lax.axis_index(CHIP) * cores + lax.axis_index("c")
    model_width = w_out.shape[1]
    kv_width = KV_HEADS * HEAD
    groups = HEADS // KV_HEADS
    tree = parents.shape[1]
    places_dev = cache_keys.shape[1]
    inputs = hidden.astype(jnp.float32)
    all_rows = inputs.shape[0]
    own_count = all_rows // tp_count
    proj_width = w_qkv.shape[1]

    scaled = (inputs * norm_gain.astype(jnp.float32)[None, :]).astype(jnp.bfloat16)
    local_squares = jnp.sum(inputs * inputs, axis=1)
    partial = jnp.dot(scaled, w_qkv, preferred_element_type=jnp.float32)
    extended = jnp.concatenate(
        [partial, jnp.broadcast_to(local_squares[:, None], (all_rows, 128))], axis=1
    )
    by_core = extended.reshape(tp_count // cores, cores, own_count, proj_width + 128)
    chip_sum = jnp.sum(lax.all_to_all(by_core, "c", 1, 1, tiled=True), axis=1)
    gathered = lax.all_to_all(chip_sum, CHIP, 0, 0, tiled=True)
    own_sum = jnp.sum(gathered, axis=0)
    square_sum = own_sum[:, proj_width]
    own_qkv = (
        own_sum[:, :proj_width] * lax.rsqrt(square_sum / model_width + 1e-05)[:, None]
    ).astype(jnp.bfloat16)
    own_queries = own_qkv[:, :model_width]
    lanes = own_count * model_width // 128
    chips = tp_count // cores
    chip_rows = lax.all_to_all(
        jnp.broadcast_to(own_queries.reshape(1, lanes, 128), (chips, lanes, 128)), CHIP, 0, 0, tiled=True
    )
    core_rows = lax.all_to_all(
        jnp.broadcast_to(chip_rows[None], (cores, chips, lanes, 128)), "c", 0, 0, tiled=True
    )
    query = jnp.swapaxes(core_rows, 0, 1).reshape(all_rows, model_width)
    own_tokens = own_qkv[:, model_width:]
    own_keys = own_tokens[:, :kv_width].reshape(own_count, KV_HEADS, HEAD)
    own_values = own_tokens[:, kv_width:].reshape(own_count, KV_HEADS, HEAD)

    scale = HEAD ** (-0.5)
    key_index = tp_rank * own_count + jnp.arange(own_count, dtype=jnp.int32)
    key_place = key_index % tree
    reached = tree_reach(parents).reshape(all_rows, tree)
    column_pick = (jnp.arange(tree, dtype=jnp.int32)[:, None] == key_place[None, :]).astype(
        jnp.float32
    )
    on_path = jnp.dot(reached, column_pick, precision=lax.Precision.HIGHEST) > 0.5
    tree_mask = on_path & (key_place < draft_counts[0])[None, :]

    query_heads = query.reshape(all_rows, KV_HEADS, groups, HEAD)
    limit = (cache_lengths[:1] - tp_rank * places_dev).astype(jnp.int32)
    head_rows = jnp.transpose(query_heads, (1, 2, 0, 3)).reshape(KV_HEADS, groups * all_rows, HEAD)
    tree_valid = jnp.broadcast_to(
        tree_mask[:, 0].astype(jnp.float32)[None, None, None, :], (KV_HEADS, 1, groups, all_rows)
    ).reshape(KV_HEADS, 1, groups * all_rows)
    cache_mixed, top_parts, total_parts, tree_weight = local_attention(
        limit,
        head_rows,
        cache_keys[0],
        cache_values[0],
        jnp.broadcast_to(own_keys[0][:, None, :], (KV_HEADS, 8, HEAD)),
        tree_valid,
    )
    head_mixed = cache_mixed + jnp.swapaxes(tree_weight, 1, 2) * own_values[0].reshape(
        KV_HEADS, 1, HEAD
    ).astype(jnp.float32)
    local_top = top_parts.reshape(HEADS, all_rows)
    totals = total_parts.reshape(HEADS, all_rows)

    columns = w_out.shape[0]
    per_head = HEAD // columns
    halves = HEAD // columns
    owner_mixed = jnp.swapaxes(
        head_mixed.reshape(HEADS, all_rows, halves, columns), 1, 2
    ).reshape(tp_count, all_rows * columns)
    owner_top = jnp.repeat(local_top, per_head, 0)
    owner_totals = jnp.repeat(totals, per_head, 0)
    packed = jnp.concatenate(
        [owner_mixed.astype(jnp.bfloat16)]
        + split3(owner_top)
        + split3(owner_totals)
        + [jnp.zeros((tp_count, 128 - (6 * all_rows) % 128), jnp.bfloat16)],
        axis=1,
    )
    got = spread(packed.reshape(tp_count, -1, 128)).reshape(tp_count, -1)
    flat = all_rows * columns
    piece = [got[:, flat + i * all_rows : flat + (i + 1) * all_rows] for i in range(6)]
    source_top = join3(*piece[:3])
    top = jnp.max(source_top, axis=0)
    rescale = jnp.exp(source_top - top[None])
    total = jnp.sum(rescale * join3(*piece[3:]), axis=0)
    source_mixed = got[:, :flat].reshape(tp_count, all_rows, columns).astype(jnp.float32)
    mixed_cols = jnp.einsum(
        "st,stc->tc", rescale, source_mixed, precision=lax.Precision.HIGHEST
    )
    attended = (mixed_cols / total[:, None]).astype(jnp.bfloat16)

    partial_terms = jnp.dot(attended, w_out, preferred_element_type=jnp.float32)
    out_cols = model_width // tp_count
    owner_terms = jnp.swapaxes(partial_terms.reshape(all_rows, tp_count, out_cols), 0, 1)
    by_core = owner_terms.reshape(chips, cores, all_rows * out_cols)
    chip_terms = jnp.sum(lax.all_to_all(by_core, "c", 1, 1, tiled=True), axis=1)
    terms = lax.all_to_all(
        chip_terms.reshape(chips, all_rows * out_cols // 128, 128).astype(jnp.bfloat16),
        CHIP,
        0,
        0,
        tiled=True,
    )
    projected = jnp.sum(terms.astype(jnp.float32), axis=0).reshape(all_rows, out_cols)
    return (inputs + projected).astype(jnp.bfloat16)


def solution(mesh):
    tp = mesh.shape["tp"]
    split = Mesh(mesh.devices.reshape(mesh.shape["req"], tp // 8, 4, 2), ("req",) + TP)
    placed = (
        P("req", TP),
        P(TP),
        P(TP, None),
        P(TP, None),
        P("req", TP, None),
        P("req", TP, None),
        P("req", None),
        P("req"),
        P("req"),
    )
    return jax.shard_map(
        on_device, mesh=split, in_specs=placed, out_specs=P("req", TP), check_vma=False
    )
```

```python
import jax
import jax.numpy as jnp
from jax import lax
from jax.experimental import pallas as pl
from jax.experimental.pallas import tpu as pltpu
from jax.sharding import Mesh
from jax.sharding import PartitionSpec as P

HEADS = 32
KV_HEADS = 4
HEAD = 128
TP = ("z", "y", "c")
CHIP = ("z", "y")


NEGATIVE = -1e30


def tree_reach(parents):
    width = parents.shape[1]
    places = jnp.arange(width, dtype=jnp.int32)
    parent_link = (parents[:, :, None] == places[None, None, :]).astype(jnp.float32)
    identity = (places[:, None] == places[None, :]).astype(jnp.float32)
    reached = jnp.minimum(parent_link + identity[None], 1.0)
    for rounds in range(width.bit_length()):
        reached = jnp.minimum(
            jnp.einsum("rij,rjk->rik", reached, reached, precision=lax.Precision.HIGHEST), 1.0
        )
    return reached


def attention_kernel(limit_ref, q_ref, k_ref, v_ref, tk_ref, tb_ref, o_ref, m_ref, l_ref, w_ref):
    rows, places = q_ref.shape[1], k_ref.shape[0]
    scale = HEAD ** (-0.5)
    query = q_ref[0]
    scores = (
        lax.dot_general(
            k_ref[...], query, (((1,), (1,)), ((), ())), preferred_element_type=jnp.float32
        )
        * scale
    )
    position = lax.broadcasted_iota(jnp.int32, (places, 1), 0)
    scores = scores + jnp.where(position < limit_ref[0], 0.0, NEGATIVE)
    own_scores = lax.dot_general(
        tk_ref[0], query, (((1,), (1,)), ((), ())), preferred_element_type=jnp.float32
    )
    tree_score = jnp.where(tb_ref[0] > 0.5, own_scores[0:1, :] * scale, NEGATIVE)
    top = jnp.maximum(jnp.max(scores, axis=0, keepdims=True), tree_score)
    shift = jnp.where(top > 0.5 * NEGATIVE, top, 0.0)
    weights = jnp.exp(scores - shift)
    tree_weight = jnp.exp(tree_score - shift)
    m_ref[0] = top
    l_ref[0] = jnp.sum(weights, axis=0, keepdims=True) + tree_weight
    w_ref[0] = tree_weight.astype(jnp.bfloat16).astype(jnp.float32)
    o_ref[0] = lax.dot_general(
        weights.astype(jnp.bfloat16),
        v_ref[...],
        (((0,), (0,)), ((), ())),
        preferred_element_type=jnp.float32,
    )


def local_attention(limit, query, keys, values, tree_keys, tree_valid):
    rows = query.shape[1]
    places = keys.shape[0]
    lane_row = pl.BlockSpec((1, 1, rows), lambda k, lim: (k, 0, 0))
    return pl.pallas_call(
        attention_kernel,
        grid_spec=pltpu.PrefetchScalarGridSpec(
            num_scalar_prefetch=1,
            grid=(KV_HEADS,),
            in_specs=[
                pl.BlockSpec((1, rows, HEAD), lambda k, lim: (k, 0, 0)),
                pl.BlockSpec((places, HEAD), lambda k, lim: (0, k)),
                pl.BlockSpec((places, HEAD), lambda k, lim: (0, k)),
                pl.BlockSpec((1, 8, HEAD), lambda k, lim: (k, 0, 0)),
                lane_row,
            ],
            out_specs=[
                pl.BlockSpec((1, rows, HEAD), lambda k, lim: (k, 0, 0)),
                lane_row,
                lane_row,
                lane_row,
            ],
        ),
        out_shape=[jax.ShapeDtypeStruct((KV_HEADS, rows, HEAD), jnp.float32)]
        + [jax.ShapeDtypeStruct((KV_HEADS, 1, rows), jnp.float32)] * 3,
    )(limit, query, keys, values, tree_keys, tree_valid)


def split3(values):
    high = lax.reduce_precision(values, exponent_bits=8, mantissa_bits=7)
    rest = values - high
    middle = lax.reduce_precision(rest, exponent_bits=8, mantissa_bits=7)
    low = rest - middle
    return [high.astype(jnp.bfloat16), middle.astype(jnp.bfloat16), low.astype(jnp.bfloat16)]


def join3(high, middle, low):
    return high.astype(jnp.float32) + middle.astype(jnp.float32) + low.astype(jnp.float32)


def spread(pieces):
    return lax.all_to_all(pieces, TP, 0, 0, tiled=True)


def on_device(
    hidden, norm_gain, w_qkv, w_out, cache_keys, cache_values, parents, draft_counts, cache_lengths
):
    cores = lax.axis_size("c")
    tp_count = lax.axis_size(CHIP) * cores
    tp_rank = lax.axis_index(CHIP) * cores + lax.axis_index("c")
    model_width = w_out.shape[1]
    kv_width = KV_HEADS * HEAD
    groups = HEADS // KV_HEADS
    tree = parents.shape[1]
    places_dev = cache_keys.shape[1]
    inputs = hidden.astype(jnp.float32)
    all_rows = inputs.shape[0]
    own_count = all_rows // tp_count
    proj_width = w_qkv.shape[1]

    scaled = (inputs * norm_gain.astype(jnp.float32)[None, :]).astype(jnp.bfloat16)
    local_squares = jnp.sum(inputs * inputs, axis=1)
    partial = jnp.dot(scaled, w_qkv, preferred_element_type=jnp.float32)
    extended = jnp.concatenate(
        [partial, jnp.broadcast_to(local_squares[:, None], (all_rows, 128))], axis=1
    )
    by_core = extended.reshape(tp_count // cores, cores, own_count, proj_width + 128)
    chip_sum = jnp.sum(lax.all_to_all(by_core, "c", 1, 1, tiled=True), axis=1)
    gathered = lax.all_to_all(chip_sum, CHIP, 0, 0, tiled=True)
    own_sum = jnp.sum(gathered, axis=0)
    square_sum = own_sum[:, proj_width]
    own_qkv = (
        own_sum[:, :proj_width] * lax.rsqrt(square_sum / model_width + 1e-05)[:, None]
    ).astype(jnp.bfloat16)
    own_queries = own_qkv[:, :model_width]
    lanes = own_count * model_width // 128
    chips = tp_count // cores
    chip_rows = lax.all_to_all(
        jnp.broadcast_to(own_queries.reshape(1, lanes, 128), (chips, lanes, 128)), CHIP, 0, 0, tiled=True
    )
    core_rows = lax.all_to_all(
        jnp.broadcast_to(chip_rows[None], (cores, chips, lanes, 128)), "c", 0, 0, tiled=True
    )
    query = jnp.swapaxes(core_rows, 0, 1).reshape(all_rows, model_width)
    own_tokens = own_qkv[:, model_width:]
    own_keys = own_tokens[:, :kv_width].reshape(own_count, KV_HEADS, HEAD)
    own_values = own_tokens[:, kv_width:].reshape(own_count, KV_HEADS, HEAD)

    scale = HEAD ** (-0.5)
    key_index = tp_rank * own_count + jnp.arange(own_count, dtype=jnp.int32)
    key_place = key_index % tree
    reached = tree_reach(parents).reshape(all_rows, tree)
    column_pick = (jnp.arange(tree, dtype=jnp.int32)[:, None] == key_place[None, :]).astype(
        jnp.float32
    )
    on_path = jnp.dot(reached, column_pick, precision=lax.Precision.HIGHEST) > 0.5
    tree_mask = on_path & (key_place < draft_counts[0])[None, :]

    query_heads = query.reshape(all_rows, KV_HEADS, groups, HEAD)
    limit = (cache_lengths[:1] - tp_rank * places_dev).astype(jnp.int32)
    head_rows = jnp.transpose(query_heads, (1, 2, 0, 3)).reshape(KV_HEADS, groups * all_rows, HEAD)
    tree_valid = jnp.broadcast_to(
        tree_mask[:, 0].astype(jnp.float32)[None, None, None, :], (KV_HEADS, 1, groups, all_rows)
    ).reshape(KV_HEADS, 1, groups * all_rows)
    cache_mixed, top_parts, total_parts, tree_weight = local_attention(
        limit,
        head_rows,
        cache_keys[0],
        cache_values[0],
        jnp.broadcast_to(own_keys[0][:, None, :], (KV_HEADS, 8, HEAD)),
        tree_valid,
    )
    head_mixed = cache_mixed + jnp.swapaxes(tree_weight, 1, 2) * own_values[0].reshape(
        KV_HEADS, 1, HEAD
    ).astype(jnp.float32)
    local_top = top_parts.reshape(HEADS, all_rows)
    totals = total_parts.reshape(HEADS, all_rows)

    columns = w_out.shape[0]
    per_head = HEAD // columns
    halves = HEAD // columns
    owner_mixed = jnp.swapaxes(
        head_mixed.reshape(HEADS, all_rows, halves, columns), 1, 2
    ).reshape(tp_count, all_rows * columns)
    owner_top = jnp.repeat(local_top, per_head, 0)
    owner_totals = jnp.repeat(totals, per_head, 0)
    packed = jnp.concatenate(
        [owner_mixed.astype(jnp.bfloat16)]
        + split3(owner_top)
        + split3(owner_totals)
        + [jnp.zeros((tp_count, 128 - (6 * all_rows) % 128), jnp.bfloat16)],
        axis=1,
    )
    got = spread(packed.reshape(tp_count, -1, 128)).reshape(tp_count, -1)
    flat = all_rows * columns
    piece = [got[:, flat + i * all_rows : flat + (i + 1) * all_rows] for i in range(6)]
    source_top = join3(*piece[:3])
    top = jnp.max(source_top, axis=0)
    rescale = jnp.exp(source_top - top[None])
    total = jnp.sum(rescale * join3(*piece[3:]), axis=0)
    source_mixed = got[:, :flat].reshape(tp_count, all_rows, columns).astype(jnp.float32)
    mixed_cols = jnp.einsum(
        "st,stc->tc", rescale, source_mixed, precision=lax.Precision.HIGHEST
    )
    attended = (mixed_cols / total[:, None]).astype(jnp.bfloat16)

    partial_terms = jnp.dot(attended, w_out, preferred_element_type=jnp.float32)
    out_cols = model_width // tp_count
    owner_terms = jnp.swapaxes(partial_terms.reshape(all_rows, tp_count, out_cols), 0, 1)
    terms = spread(
        owner_terms.reshape(tp_count, all_rows * out_cols // 128, 128).astype(jnp.bfloat16)
    )
    projected = jnp.sum(terms.astype(jnp.float32), axis=0).reshape(all_rows, out_cols)
    return (inputs + projected).astype(jnp.bfloat16)


def solution(mesh):
    tp = mesh.shape["tp"]
    split = Mesh(mesh.devices.reshape(mesh.shape["req"], tp // 8, 4, 2), ("req",) + TP)
    placed = (
        P("req", TP),
        P(TP),
        P(TP, None),
        P(TP, None),
        P("req", TP, None),
        P("req", TP, None),
        P("req", None),
        P("req"),
        P("req"),
    )
    return jax.shard_map(
        on_device, mesh=split, in_specs=placed, out_specs=P("req", TP), check_vma=False
    )
```

```python
import jax
import jax.numpy as jnp
from jax import lax
from jax.experimental import pallas as pl
from jax.experimental.pallas import tpu as pltpu
from jax.sharding import Mesh
from jax.sharding import PartitionSpec as P

HEADS = 32
KV_HEADS = 4
HEAD = 128
TP = ("z", "y", "c")
CHIP = ("z", "y")


NEGATIVE = -1e30


def tree_reach(parents):
    width = parents.shape[1]
    places = jnp.arange(width, dtype=jnp.int32)
    parent_link = (parents[:, :, None] == places[None, None, :]).astype(jnp.float32)
    identity = (places[:, None] == places[None, :]).astype(jnp.float32)
    reached = jnp.minimum(parent_link + identity[None], 1.0)
    for rounds in range(width.bit_length()):
        reached = jnp.minimum(
            jnp.einsum("rij,rjk->rik", reached, reached, precision=lax.Precision.HIGHEST), 1.0
        )
    return reached


def attention_kernel(limit_ref, q_ref, k_ref, v_ref, tk_ref, tb_ref, o_ref, m_ref, l_ref, w_ref):
    rows, places = q_ref.shape[1], k_ref.shape[0]
    scale = HEAD ** (-0.5)
    query = q_ref[0]
    scores = (
        lax.dot_general(
            k_ref[...], query, (((1,), (1,)), ((), ())), preferred_element_type=jnp.float32
        )
        * scale
    )
    position = lax.broadcasted_iota(jnp.int32, (places, 1), 0)
    scores = scores + jnp.where(position < limit_ref[0], 0.0, NEGATIVE)
    own_scores = lax.dot_general(
        tk_ref[0], query, (((1,), (1,)), ((), ())), preferred_element_type=jnp.float32
    )
    tree_score = jnp.where(tb_ref[0] > 0.5, own_scores[0:1, :] * scale, NEGATIVE)
    top = jnp.maximum(jnp.max(scores, axis=0, keepdims=True), tree_score)
    shift = jnp.where(top > 0.5 * NEGATIVE, top, 0.0)
    weights = jnp.exp(scores - shift)
    tree_weight = jnp.exp(tree_score - shift)
    m_ref[0] = top
    l_ref[0] = jnp.sum(weights, axis=0, keepdims=True) + tree_weight
    w_ref[0] = tree_weight.astype(jnp.bfloat16).astype(jnp.float32)
    o_ref[0] = lax.dot_general(
        weights.astype(jnp.bfloat16),
        v_ref[...],
        (((0,), (0,)), ((), ())),
        preferred_element_type=jnp.float32,
    )


def local_attention(limit, query, keys, values, tree_keys, tree_valid):
    rows = query.shape[1]
    places = keys.shape[0]
    lane_row = pl.BlockSpec((1, 1, rows), lambda k, lim: (k, 0, 0))
    return pl.pallas_call(
        attention_kernel,
        grid_spec=pltpu.PrefetchScalarGridSpec(
            num_scalar_prefetch=1,
            grid=(KV_HEADS,),
            in_specs=[
                pl.BlockSpec((1, rows, HEAD), lambda k, lim: (k, 0, 0)),
                pl.BlockSpec((places, HEAD), lambda k, lim: (0, k)),
                pl.BlockSpec((places, HEAD), lambda k, lim: (0, k)),
                pl.BlockSpec((1, 8, HEAD), lambda k, lim: (k, 0, 0)),
                lane_row,
            ],
            out_specs=[
                pl.BlockSpec((1, rows, HEAD), lambda k, lim: (k, 0, 0)),
                lane_row,
                lane_row,
                lane_row,
            ],
        ),
        out_shape=[jax.ShapeDtypeStruct((KV_HEADS, rows, HEAD), jnp.float32)]
        + [jax.ShapeDtypeStruct((KV_HEADS, 1, rows), jnp.float32)] * 3,
    )(limit, query, keys, values, tree_keys, tree_valid)


def split3(values):
    high = lax.reduce_precision(values, exponent_bits=8, mantissa_bits=7)
    rest = values - high
    middle = lax.reduce_precision(rest, exponent_bits=8, mantissa_bits=7)
    low = rest - middle
    return [high.astype(jnp.bfloat16), middle.astype(jnp.bfloat16), low.astype(jnp.bfloat16)]


def join3(high, middle, low):
    return high.astype(jnp.float32) + middle.astype(jnp.float32) + low.astype(jnp.float32)


def spread(pieces):
    return lax.all_to_all(pieces, TP, 0, 0, tiled=True)


def on_device(
    hidden, norm_gain, w_qkv, w_out, cache_keys, cache_values, parents, draft_counts, cache_lengths
):
    cores = lax.axis_size("c")
    tp_count = lax.axis_size(CHIP) * cores
    tp_rank = lax.axis_index(CHIP) * cores + lax.axis_index("c")
    model_width = w_out.shape[1]
    kv_width = KV_HEADS * HEAD
    groups = HEADS // KV_HEADS
    tree = parents.shape[1]
    places_dev = cache_keys.shape[1]
    inputs = hidden.astype(jnp.float32)
    all_rows = inputs.shape[0]
    own_count = all_rows // tp_count
    proj_width = w_qkv.shape[1]

    scaled = (inputs * norm_gain.astype(jnp.float32)[None, :]).astype(jnp.bfloat16)
    local_squares = jnp.sum(inputs * inputs, axis=1)
    partial = jnp.dot(scaled, w_qkv, preferred_element_type=jnp.float32)
    extended = jnp.concatenate(
        [partial, jnp.broadcast_to(local_squares[:, None], (all_rows, 128))], axis=1
    )
    by_core = extended.reshape(tp_count // cores, cores, own_count, proj_width + 128)
    chip_sum = jnp.sum(lax.all_to_all(by_core, "c", 1, 1, tiled=True), axis=1)
    gathered = lax.all_to_all(chip_sum, CHIP, 0, 0, tiled=True)
    own_sum = jnp.sum(gathered, axis=0)
    square_sum = own_sum[:, proj_width]
    own_qkv = (
        own_sum[:, :proj_width] * lax.rsqrt(square_sum / model_width + 1e-05)[:, None]
    ).astype(jnp.bfloat16)
    own_queries = own_qkv[:, :model_width]
    lanes = own_count * model_width // 128
    chips = tp_count // cores
    chip_rows = lax.all_to_all(
        jnp.broadcast_to(own_queries.reshape(1, lanes, 128), (chips, lanes, 128)), CHIP, 0, 0, tiled=True
    )
    core_rows = lax.all_to_all(
        jnp.broadcast_to(chip_rows[None], (cores, chips, lanes, 128)), "c", 0, 0, tiled=True
    )
    query = jnp.swapaxes(core_rows, 0, 1).reshape(all_rows, model_width)
    own_tokens = own_qkv[:, model_width:]
    own_keys = own_tokens[:, :kv_width].reshape(own_count, KV_HEADS, HEAD)
    own_values = own_tokens[:, kv_width:].reshape(own_count, KV_HEADS, HEAD)

    scale = HEAD ** (-0.5)
    key_index = tp_rank * own_count + jnp.arange(own_count, dtype=jnp.int32)
    key_place = key_index % tree
    reached = tree_reach(parents).reshape(all_rows, tree)
    column_pick = (jnp.arange(tree, dtype=jnp.int32)[:, None] == key_place[None, :]).astype(
        jnp.float32
    )
    on_path = jnp.dot(reached, column_pick, precision=lax.Precision.HIGHEST) > 0.5
    tree_mask = on_path & (key_place < draft_counts[0])[None, :]

    query_heads = query.reshape(all_rows, KV_HEADS, groups, HEAD)
    limit = (cache_lengths[:1] - tp_rank * places_dev).astype(jnp.int32)
    head_rows = jnp.transpose(query_heads, (1, 2, 0, 3)).reshape(KV_HEADS, groups * all_rows, HEAD)
    tree_valid = jnp.broadcast_to(
        tree_mask[:, 0].astype(jnp.float32)[None, None, None, :], (KV_HEADS, 1, groups, all_rows)
    ).reshape(KV_HEADS, 1, groups * all_rows)
    cache_mixed, top_parts, total_parts, tree_weight = local_attention(
        limit,
        head_rows,
        cache_keys[0],
        cache_values[0],
        jnp.broadcast_to(own_keys[0][:, None, :], (KV_HEADS, 8, HEAD)),
        tree_valid,
    )
    head_mixed = cache_mixed + jnp.swapaxes(tree_weight, 1, 2) * own_values[0].reshape(
        KV_HEADS, 1, HEAD
    ).astype(jnp.float32)
    local_top = top_parts.reshape(HEADS, all_rows)
    totals = total_parts.reshape(HEADS, all_rows)

    columns = w_out.shape[0]
    per_head = HEAD // columns
    halves = HEAD // columns
    owner_mixed = jnp.swapaxes(
        head_mixed.reshape(HEADS, all_rows, halves, columns), 1, 2
    ).reshape(tp_count, all_rows * columns)
    owner_top = jnp.repeat(local_top, per_head, 0)
    owner_totals = jnp.repeat(totals, per_head, 0)
    packed = jnp.concatenate(
        [owner_mixed.astype(jnp.bfloat16)]
        + split3(owner_top)
        + split3(owner_totals)
        + [jnp.zeros((tp_count, 128 - (6 * all_rows) % 128), jnp.bfloat16)],
        axis=1,
    )
    got = spread(packed.reshape(tp_count, -1, 128)).reshape(tp_count, -1)
    flat = all_rows * columns
    piece = [got[:, flat + i * all_rows : flat + (i + 1) * all_rows] for i in range(6)]
    source_top = join3(*piece[:3])
    top = jnp.max(source_top, axis=0)
    rescale = jnp.exp(source_top - top[None])
    total = jnp.sum(rescale * join3(*piece[3:]), axis=0)
    source_mixed = got[:, :flat].reshape(tp_count, all_rows, columns).astype(jnp.float32)
    mixed_cols = jnp.einsum(
        "st,stc->tc", rescale, source_mixed, precision=lax.Precision.HIGHEST
    )
    attended = (mixed_cols / total[:, None]).astype(jnp.bfloat16)

    partial_terms = jnp.dot(attended, w_out, preferred_element_type=jnp.float32)
    out_cols = model_width // tp_count
    by_core = jnp.transpose(
        partial_terms.reshape(all_rows, chips, cores, out_cols), (2, 1, 0, 3)
    ).reshape(cores, chips, all_rows * out_cols // 128, 128)
    chip_terms = jnp.sum(lax.all_to_all(by_core, "c", 0, 0, tiled=True), axis=0)
    terms = lax.all_to_all(chip_terms.astype(jnp.bfloat16), CHIP, 0, 0, tiled=True)
    projected = jnp.sum(terms.astype(jnp.float32), axis=0).reshape(all_rows, out_cols)
    return (inputs + projected).astype(jnp.bfloat16)


def solution(mesh):
    tp = mesh.shape["tp"]
    split = Mesh(mesh.devices.reshape(mesh.shape["req"], tp // 8, 4, 2), ("req",) + TP)
    placed = (
        P("req", TP),
        P(TP),
        P(TP, None),
        P(TP, None),
        P("req", TP, None),
        P("req", TP, None),
        P("req", None),
        P("req"),
        P("req"),
    )
    return jax.shard_map(
        on_device, mesh=split, in_specs=placed, out_specs=P("req", TP), check_vma=False
    )
```

```python
import jax
import jax.numpy as jnp
from jax import lax
from jax.experimental import pallas as pl
from jax.experimental.pallas import tpu as pltpu
from jax.sharding import Mesh
from jax.sharding import PartitionSpec as P

HEADS = 32
KV_HEADS = 4
HEAD = 128
TP = ("z", "y", "c")
CHIP = ("z", "y")


NEGATIVE = -1e30


def tree_reach(parents):
    width = parents.shape[1]
    places = jnp.arange(width, dtype=jnp.int32)
    parent_link = (parents[:, :, None] == places[None, None, :]).astype(jnp.float32)
    identity = (places[:, None] == places[None, :]).astype(jnp.float32)
    reached = jnp.minimum(parent_link + identity[None], 1.0)
    for rounds in range(width.bit_length()):
        reached = jnp.minimum(
            jnp.einsum("rij,rjk->rik", reached, reached, precision=lax.Precision.HIGHEST), 1.0
        )
    return reached


def attention_kernel(limit_ref, q_ref, k_ref, v_ref, tk_ref, tb_ref, o_ref, m_ref, l_ref, w_ref):
    rows, places = q_ref.shape[0] * q_ref.shape[1], k_ref.shape[0]
    scale = HEAD ** (-0.5)
    query = q_ref[...].reshape(rows, HEAD)
    scores = (
        lax.dot_general(
            k_ref[...], query, (((1,), (1,)), ((), ())), preferred_element_type=jnp.float32
        )
        * scale
    )
    position = lax.broadcasted_iota(jnp.int32, (places, 1), 0)
    scores = scores + jnp.where(position < limit_ref[0], 0.0, NEGATIVE)
    own_scores = lax.dot_general(
        tk_ref[0], query, (((1,), (1,)), ((), ())), preferred_element_type=jnp.float32
    )
    tree_score = jnp.where(tb_ref[0] > 0.5, own_scores[0:1, :] * scale, NEGATIVE)
    top = jnp.maximum(jnp.max(scores, axis=0, keepdims=True), tree_score)
    shift = jnp.where(top > 0.5 * NEGATIVE, top, 0.0)
    weights = jnp.exp(scores - shift)
    tree_weight = jnp.exp(tree_score - shift)
    m_ref[0] = top
    l_ref[0] = jnp.sum(weights, axis=0, keepdims=True) + tree_weight
    w_ref[0] = tree_weight.astype(jnp.bfloat16).astype(jnp.float32)
    o_ref[0] = lax.dot_general(
        weights.astype(jnp.bfloat16),
        v_ref[...],
        (((0,), (0,)), ((), ())),
        preferred_element_type=jnp.float32,
    )


def local_attention(limit, query, keys, values, tree_keys, tree_valid):
    tokens, groups = query.shape[0], HEADS // KV_HEADS
    rows = tokens * groups
    places = keys.shape[0]
    lane_row = pl.BlockSpec((1, 1, rows), lambda k, lim: (k, 0, 0))
    return pl.pallas_call(
        attention_kernel,
        grid_spec=pltpu.PrefetchScalarGridSpec(
            num_scalar_prefetch=1,
            grid=(KV_HEADS,),
            in_specs=[
                pl.BlockSpec((tokens, groups, HEAD), lambda k, lim: (0, k, 0)),
                pl.BlockSpec((places, HEAD), lambda k, lim: (0, k)),
                pl.BlockSpec((places, HEAD), lambda k, lim: (0, k)),
                pl.BlockSpec((1, 8, HEAD), lambda k, lim: (k, 0, 0)),
                lane_row,
            ],
            out_specs=[
                pl.BlockSpec((1, rows, HEAD), lambda k, lim: (k, 0, 0)),
                lane_row,
                lane_row,
                lane_row,
            ],
        ),
        out_shape=[jax.ShapeDtypeStruct((KV_HEADS, rows, HEAD), jnp.float32)]
        + [jax.ShapeDtypeStruct((KV_HEADS, 1, rows), jnp.float32)] * 3,
    )(limit, query, keys, values, tree_keys, tree_valid)


def split3(values):
    high = lax.reduce_precision(values, exponent_bits=8, mantissa_bits=7)
    rest = values - high
    middle = lax.reduce_precision(rest, exponent_bits=8, mantissa_bits=7)
    low = rest - middle
    return [high.astype(jnp.bfloat16), middle.astype(jnp.bfloat16), low.astype(jnp.bfloat16)]


def join3(high, middle, low):
    return high.astype(jnp.float32) + middle.astype(jnp.float32) + low.astype(jnp.float32)


def spread(pieces):
    return lax.all_to_all(pieces, TP, 0, 0, tiled=True)


def on_device(
    hidden, norm_gain, w_qkv, w_out, cache_keys, cache_values, parents, draft_counts, cache_lengths
):
    cores = lax.axis_size("c")
    tp_count = lax.axis_size(CHIP) * cores
    tp_rank = lax.axis_index(CHIP) * cores + lax.axis_index("c")
    model_width = w_out.shape[1]
    kv_width = KV_HEADS * HEAD
    groups = HEADS // KV_HEADS
    tree = parents.shape[1]
    places_dev = cache_keys.shape[1]
    inputs = hidden.astype(jnp.float32)
    all_rows = inputs.shape[0]
    own_count = all_rows // tp_count
    proj_width = w_qkv.shape[1]

    scaled = (inputs * norm_gain.astype(jnp.float32)[None, :]).astype(jnp.bfloat16)
    local_squares = jnp.sum(inputs * inputs, axis=1)
    partial = jnp.dot(scaled, w_qkv, preferred_element_type=jnp.float32)
    extended = jnp.concatenate(
        [partial, jnp.broadcast_to(local_squares[:, None], (all_rows, 128))], axis=1
    )
    by_core = extended.reshape(tp_count // cores, cores, own_count, proj_width + 128)
    chip_sum = jnp.sum(lax.all_to_all(by_core, "c", 1, 1, tiled=True), axis=1)
    gathered = lax.all_to_all(chip_sum, CHIP, 0, 0, tiled=True)
    own_sum = jnp.sum(gathered, axis=0)
    square_sum = own_sum[:, proj_width]
    own_qkv = (
        own_sum[:, :proj_width] * lax.rsqrt(square_sum / model_width + 1e-05)[:, None]
    ).astype(jnp.bfloat16)
    own_queries = own_qkv[:, :model_width]
    lanes = own_count * model_width // 128
    chips = tp_count // cores
    chip_rows = lax.all_to_all(
        jnp.broadcast_to(own_queries.reshape(1, lanes, 128), (chips, lanes, 128)), CHIP, 0, 0, tiled=True
    )
    core_rows = lax.all_to_all(
        jnp.broadcast_to(chip_rows[None], (cores, chips, lanes, 128)), "c", 0, 0, tiled=True
    )
    query = core_rows.reshape(all_rows, HEADS, HEAD)
    own_tokens = own_qkv[:, model_width:]
    own_keys = own_tokens[:, :kv_width].reshape(own_count, KV_HEADS, HEAD)
    own_values = own_tokens[:, kv_width:].reshape(own_count, KV_HEADS, HEAD)

    scale = HEAD ** (-0.5)
    key_index = tp_rank * own_count + jnp.arange(own_count, dtype=jnp.int32)
    key_place = key_index % tree
    reached = tree_reach(parents).reshape(all_rows, tree)
    column_pick = (jnp.arange(tree, dtype=jnp.int32)[:, None] == key_place[None, :]).astype(
        jnp.float32
    )
    on_path = jnp.dot(reached, column_pick, precision=lax.Precision.HIGHEST) > 0.5
    tree_mask = on_path & (key_place < draft_counts[0])[None, :]

    limit = (cache_lengths[:1] - tp_rank * places_dev).astype(jnp.int32)
    valid_rows = jnp.swapaxes(tree_mask[:, 0].astype(jnp.float32).reshape(chips, cores), 0, 1)
    tree_valid = jnp.broadcast_to(
        valid_rows[None, None, :, :, None], (KV_HEADS, 1, cores, chips, groups)
    ).reshape(KV_HEADS, 1, groups * all_rows)
    cache_mixed, top_parts, total_parts, tree_weight = local_attention(
        limit,
        query,
        cache_keys[0],
        cache_values[0],
        jnp.broadcast_to(own_keys[0][:, None, :], (KV_HEADS, 8, HEAD)),
        tree_valid,
    )
    row_mixed = cache_mixed + jnp.swapaxes(tree_weight, 1, 2) * own_values[0].reshape(
        KV_HEADS, 1, HEAD
    ).astype(jnp.float32)
    head_mixed = jnp.transpose(
        row_mixed.reshape(KV_HEADS, cores, chips, groups, HEAD), (0, 3, 2, 1, 4)
    ).reshape(HEADS, all_rows, HEAD)
    local_top = jnp.transpose(
        top_parts.reshape(KV_HEADS, cores, chips, groups), (0, 3, 2, 1)
    ).reshape(HEADS, all_rows)
    totals = jnp.transpose(
        total_parts.reshape(KV_HEADS, cores, chips, groups), (0, 3, 2, 1)
    ).reshape(HEADS, all_rows)

    columns = w_out.shape[0]
    per_head = HEAD // columns
    halves = HEAD // columns
    owner_mixed = jnp.swapaxes(
        head_mixed.reshape(HEADS, all_rows, halves, columns), 1, 2
    ).reshape(tp_count, all_rows * columns)
    owner_top = jnp.repeat(local_top, per_head, 0)
    owner_totals = jnp.repeat(totals, per_head, 0)
    packed = jnp.concatenate(
        [owner_mixed.astype(jnp.bfloat16)]
        + split3(owner_top)
        + split3(owner_totals)
        + [jnp.zeros((tp_count, 128 - (6 * all_rows) % 128), jnp.bfloat16)],
        axis=1,
    )
    got = spread(packed.reshape(tp_count, -1, 128)).reshape(tp_count, -1)
    flat = all_rows * columns
    piece = [got[:, flat + i * all_rows : flat + (i + 1) * all_rows] for i in range(6)]
    source_top = join3(*piece[:3])
    top = jnp.max(source_top, axis=0)
    rescale = jnp.exp(source_top - top[None])
    total = jnp.sum(rescale * join3(*piece[3:]), axis=0)
    source_mixed = got[:, :flat].reshape(tp_count, all_rows, columns).astype(jnp.float32)
    mixed_cols = jnp.einsum(
        "st,stc->tc", rescale, source_mixed, precision=lax.Precision.HIGHEST
    )
    attended = (mixed_cols / total[:, None]).astype(jnp.bfloat16)

    partial_terms = jnp.dot(attended, w_out, preferred_element_type=jnp.float32)
    out_cols = model_width // tp_count
    owner_terms = jnp.swapaxes(partial_terms.reshape(all_rows, tp_count, out_cols), 0, 1)
    terms = spread(
        owner_terms.reshape(tp_count, all_rows * out_cols // 128, 128).astype(jnp.bfloat16)
    )
    projected = jnp.sum(terms.astype(jnp.float32), axis=0).reshape(all_rows, out_cols)
    return (inputs + projected).astype(jnp.bfloat16)


def solution(mesh):
    tp = mesh.shape["tp"]
    split = Mesh(mesh.devices.reshape(mesh.shape["req"], tp // 8, 4, 2), ("req",) + TP)
    placed = (
        P("req", TP),
        P(TP),
        P(TP, None),
        P(TP, None),
        P("req", TP, None),
        P("req", TP, None),
        P("req", None),
        P("req"),
        P("req"),
    )
    return jax.shard_map(
        on_device, mesh=split, in_specs=placed, out_specs=P("req", TP), check_vma=False
    )
```

```python
import jax
import jax.numpy as jnp
from jax import lax
from jax.experimental import pallas as pl
from jax.experimental.pallas import tpu as pltpu
from jax.sharding import Mesh
from jax.sharding import PartitionSpec as P

HEADS = 32
KV_HEADS = 4
HEAD = 128
TP = ("z", "y", "c")
CHIP = ("z", "y")


NEGATIVE = -1e30


def tree_reach(parents):
    width = parents.shape[1]
    places = jnp.arange(width, dtype=jnp.int32)
    parent_link = (parents[:, :, None] == places[None, None, :]).astype(jnp.float32)
    identity = (places[:, None] == places[None, :]).astype(jnp.float32)
    reached = jnp.minimum(parent_link + identity[None], 1.0)
    for rounds in range(width.bit_length()):
        reached = jnp.minimum(
            jnp.einsum("rij,rjk->rik", reached, reached, precision=lax.Precision.HIGHEST), 1.0
        )
    return reached


def attention_kernel(limit_ref, q_ref, k_ref, v_ref, tk_ref, tb_ref, o_ref, m_ref, l_ref, w_ref):
    rows, places = q_ref.shape[1], k_ref.shape[0]
    scale = HEAD ** (-0.5)
    query = q_ref[0]
    scores = (
        lax.dot_general(
            k_ref[...], query, (((1,), (1,)), ((), ())), preferred_element_type=jnp.float32
        )
        * scale
    )
    position = lax.broadcasted_iota(jnp.int32, (places, 1), 0)
    scores = scores + jnp.where(position < limit_ref[0], 0.0, NEGATIVE)
    own_scores = lax.dot_general(
        tk_ref[0], query, (((1,), (1,)), ((), ())), preferred_element_type=jnp.float32
    )
    tree_score = jnp.where(tb_ref[0] > 0.5, own_scores[0:1, :] * scale, NEGATIVE)
    top = jnp.maximum(jnp.max(scores, axis=0, keepdims=True), tree_score)
    shift = jnp.where(top > 0.5 * NEGATIVE, top, 0.0)
    weights = jnp.exp(scores - shift)
    tree_weight = jnp.exp(tree_score - shift)
    m_ref[0] = top
    l_ref[0] = jnp.sum(weights, axis=0, keepdims=True) + tree_weight
    w_ref[0] = tree_weight.astype(jnp.bfloat16).astype(jnp.float32)
    o_ref[0] = lax.dot_general(
        weights.astype(jnp.bfloat16),
        v_ref[...],
        (((0,), (0,)), ((), ())),
        preferred_element_type=jnp.float32,
    )


def local_attention(limit, query, keys, values, tree_keys, tree_valid):
    rows = query.shape[1]
    places = keys.shape[0]
    lane_row = pl.BlockSpec((1, 1, rows), lambda k, lim: (k, 0, 0))
    return pl.pallas_call(
        attention_kernel,
        grid_spec=pltpu.PrefetchScalarGridSpec(
            num_scalar_prefetch=1,
            grid=(KV_HEADS,),
            in_specs=[
                pl.BlockSpec((1, rows, HEAD), lambda k, lim: (k, 0, 0)),
                pl.BlockSpec((places, HEAD), lambda k, lim: (0, k)),
                pl.BlockSpec((places, HEAD), lambda k, lim: (0, k)),
                pl.BlockSpec((1, 8, HEAD), lambda k, lim: (k, 0, 0)),
                lane_row,
            ],
            out_specs=[
                pl.BlockSpec((1, rows, HEAD), lambda k, lim: (k, 0, 0)),
                lane_row,
                lane_row,
                lane_row,
            ],
        ),
        out_shape=[jax.ShapeDtypeStruct((KV_HEADS, rows, HEAD), jnp.float32)]
        + [jax.ShapeDtypeStruct((KV_HEADS, 1, rows), jnp.float32)] * 3,
    )(limit, query, keys, values, tree_keys, tree_valid)


def split3(values):
    high = lax.reduce_precision(values, exponent_bits=8, mantissa_bits=7)
    rest = values - high
    middle = lax.reduce_precision(rest, exponent_bits=8, mantissa_bits=7)
    low = rest - middle
    return [high.astype(jnp.bfloat16), middle.astype(jnp.bfloat16), low.astype(jnp.bfloat16)]


def split2(values):
    high = lax.reduce_precision(values, exponent_bits=8, mantissa_bits=7)
    return [high.astype(jnp.bfloat16), (values - high).astype(jnp.bfloat16)]


def join3(high, middle, low):
    return high.astype(jnp.float32) + middle.astype(jnp.float32) + low.astype(jnp.float32)


def spread(pieces):
    return lax.all_to_all(pieces, TP, 0, 0, tiled=True)


def on_device(
    hidden, norm_gain, w_qkv, w_out, cache_keys, cache_values, parents, draft_counts, cache_lengths
):
    cores = lax.axis_size("c")
    tp_count = lax.axis_size(CHIP) * cores
    tp_rank = lax.axis_index(CHIP) * cores + lax.axis_index("c")
    model_width = w_out.shape[1]
    kv_width = KV_HEADS * HEAD
    groups = HEADS // KV_HEADS
    tree = parents.shape[1]
    places_dev = cache_keys.shape[1]
    inputs = hidden.astype(jnp.float32)
    all_rows = inputs.shape[0]
    own_count = all_rows // tp_count
    proj_width = w_qkv.shape[1]

    scaled = (inputs * norm_gain.astype(jnp.float32)[None, :]).astype(jnp.bfloat16)
    local_squares = jnp.sum(inputs * inputs, axis=1)
    partial = jnp.dot(scaled, w_qkv, preferred_element_type=jnp.float32)
    extended = jnp.concatenate(
        [partial, jnp.broadcast_to(local_squares[:, None], (all_rows, 128))], axis=1
    )
    by_core = extended.reshape(tp_count // cores, cores, own_count, proj_width + 128)
    chip_sum = jnp.sum(lax.all_to_all(by_core, "c", 1, 1, tiled=True), axis=1)
    gathered = lax.all_to_all(chip_sum, CHIP, 0, 0, tiled=True)
    own_sum = jnp.sum(gathered, axis=0)
    square_sum = own_sum[:, proj_width]
    own_qkv = (
        own_sum[:, :proj_width] * lax.rsqrt(square_sum / model_width + 1e-05)[:, None]
    ).astype(jnp.bfloat16)
    own_queries = own_qkv[:, :model_width]
    lanes = own_count * model_width // 128
    chips = tp_count // cores
    chip_rows = lax.all_to_all(
        jnp.broadcast_to(own_queries.reshape(1, lanes, 128), (chips, lanes, 128)), CHIP, 0, 0, tiled=True
    )
    core_rows = lax.all_to_all(
        jnp.broadcast_to(chip_rows[None], (cores, chips, lanes, 128)), "c", 0, 0, tiled=True
    )
    query = jnp.swapaxes(core_rows, 0, 1).reshape(all_rows, model_width)
    own_tokens = own_qkv[:, model_width:]
    own_keys = own_tokens[:, :kv_width].reshape(own_count, KV_HEADS, HEAD)
    own_values = own_tokens[:, kv_width:].reshape(own_count, KV_HEADS, HEAD)

    scale = HEAD ** (-0.5)
    key_index = tp_rank * own_count + jnp.arange(own_count, dtype=jnp.int32)
    key_place = key_index % tree
    reached = tree_reach(parents).reshape(all_rows, tree)
    column_pick = (jnp.arange(tree, dtype=jnp.int32)[:, None] == key_place[None, :]).astype(
        jnp.float32
    )
    on_path = jnp.dot(reached, column_pick, precision=lax.Precision.HIGHEST) > 0.5
    tree_mask = on_path & (key_place < draft_counts[0])[None, :]

    query_heads = query.reshape(all_rows, KV_HEADS, groups, HEAD)
    limit = (cache_lengths[:1] - tp_rank * places_dev).astype(jnp.int32)
    head_rows = jnp.transpose(query_heads, (1, 2, 0, 3)).reshape(KV_HEADS, groups * all_rows, HEAD)
    tree_valid = jnp.broadcast_to(
        tree_mask[:, 0].astype(jnp.float32)[None, None, None, :], (KV_HEADS, 1, groups, all_rows)
    ).reshape(KV_HEADS, 1, groups * all_rows)
    cache_mixed, top_parts, total_parts, tree_weight = local_attention(
        limit,
        head_rows,
        cache_keys[0],
        cache_values[0],
        jnp.broadcast_to(own_keys[0][:, None, :], (KV_HEADS, 8, HEAD)),
        tree_valid,
    )
    head_mixed = cache_mixed + jnp.swapaxes(tree_weight, 1, 2) * own_values[0].reshape(
        KV_HEADS, 1, HEAD
    ).astype(jnp.float32)
    local_top = top_parts.reshape(HEADS, all_rows)
    totals = total_parts.reshape(HEADS, all_rows)

    columns = w_out.shape[0]
    per_head = HEAD // columns
    halves = HEAD // columns
    owner_mixed = jnp.swapaxes(
        head_mixed.reshape(HEADS, all_rows, halves, columns), 1, 2
    ).reshape(tp_count, all_rows * columns)
    owner_top = jnp.repeat(local_top, per_head, 0)
    owner_totals = jnp.repeat(totals, per_head, 0)
    packed = jnp.concatenate(
        [owner_mixed.astype(jnp.bfloat16)]
        + split2(owner_top)
        + split2(owner_totals),
        axis=1,
    )
    got = spread(packed.reshape(tp_count, -1, 128)).reshape(tp_count, -1)
    flat = all_rows * columns
    piece = [got[:, flat + i * all_rows : flat + (i + 1) * all_rows].astype(jnp.float32) for i in range(4)]
    source_top = piece[0] + piece[1]
    top = jnp.max(source_top, axis=0)
    rescale = jnp.exp(source_top - top[None])
    total = jnp.sum(rescale * (piece[2] + piece[3]), axis=0)
    source_mixed = got[:, :flat].reshape(tp_count, all_rows, columns).astype(jnp.float32)
    mixed_cols = jnp.einsum(
        "st,stc->tc", rescale, source_mixed, precision=lax.Precision.HIGHEST
    )
    attended = (mixed_cols / total[:, None]).astype(jnp.bfloat16)

    partial_terms = jnp.dot(attended, w_out, preferred_element_type=jnp.float32)
    out_cols = model_width // tp_count
    owner_terms = jnp.swapaxes(partial_terms.reshape(all_rows, tp_count, out_cols), 0, 1)
    terms = spread(
        owner_terms.reshape(tp_count, all_rows * out_cols // 128, 128).astype(jnp.bfloat16)
    )
    projected = jnp.sum(terms.astype(jnp.float32), axis=0).reshape(all_rows, out_cols)
    return (inputs + projected).astype(jnp.bfloat16)


def solution(mesh):
    tp = mesh.shape["tp"]
    split = Mesh(mesh.devices.reshape(mesh.shape["req"], tp // 8, 4, 2), ("req",) + TP)
    placed = (
        P("req", TP),
        P(TP),
        P(TP, None),
        P(TP, None),
        P("req", TP, None),
        P("req", TP, None),
        P("req", None),
        P("req"),
        P("req"),
    )
    return jax.shard_map(
        on_device, mesh=split, in_specs=placed, out_specs=P("req", TP), check_vma=False
    )
```
